1024 devices in a mesh: gx: 64 (over y_lo, x, core), gy: 16 (over z, y_hi).
Axes of the slice: x: 8, y: 8 (y_hi: 2, y_lo: 4; y = y_hi * 4 + y_lo), z: 8, core: 2. Of those that a mesh axis runs over, the one named last changes fastest.
Arguments:
- velocity: float32 [512, 128, 128], P('gx', 'gy'), may hold values from -6 to 6
- cotangent: float32 [512, 128, 128], P('gx', 'gy'), may hold values from -6 to 6
- block_ids: int32 [64, 16, 128], P('gx', 'gy'), may hold values from 0 to 127, as said below
- fluid_count: int32 [64, 16], P('gx', 'gy'), may hold values from 32 to 128, as said below
- fluid_cells: int32 [64, 16, 8192], P('gx', 'gy'), may hold values 0 or 1
- w_in: bfloat16 [64, 7], replicated, may hold values from -2 to 2
- w_mid: bfloat16 [64, 64], replicated, may hold values from -0.75 to 0.75
- w_out: bfloat16 [1, 64], replicated, may hold values from -0.75 to 0.75
Outputs:
- new_field: float32 [512, 128, 128], P('gx', 'gy')
- grad_field: float32 [512, 128, 128], P('gx', 'gy')
- grad_in: float32 [64, 7], replicated
- grad_mid: float32 [64, 64], replicated
- grad_out: float32 [1, 64], replicated
The draws below stay inside these ranges and needn't reach their ends.
Inputs may be any that keep to these rules, and one draw needn't show every extreme that they name: `block_ids`: within one device's list the block numbers are distinct. `fluid_count`: some device's list is wholly live.
All inputs are finite; a program needn't handle non-finite values. No bound on the sum of `fluid_cells` on one device may be relied on, other than what follows from the above.
Results may differ from the reference program's by a relative error of at most 0.018.
Values sent between devices are 32-bit elements; how exact they have to be, the bound alone decides.
No kernel may reach another device: no remote copies, remote signals or barrier semaphores. Data moves between devices by JAX's collectives and lax.ppermute only.
A program may use at most 32 MiB of HBM per device.

```python
import jax
import jax.numpy as jnp
from jax import lax

CX = 8
CY = 8
NZ = 128
BCAP = 128
CH = 64
NB = 128
NX = 512
NY = 128
N_GX = 64
N_GY = 16


def draw_block_ids(key, part):
    groups = NX // CX * (NY // CY)
    subkeys = jax.random.split(key, groups)

    def pick(subkey):
        return jax.random.permutation(subkey, NB)[:BCAP]
    chosen = jax.vmap(pick)(subkeys)
    return chosen.reshape(NX // CX, NY // CY, BCAP).astype(jnp.int32)


def draw_fluid_count(key, part):
    groups = NX // CX * (NY // CY)
    counts = jax.random.randint(jax.random.fold_in(key, 11), (groups,), max(1, BCAP // 4), BCAP + 1)
    fullest = jax.random.randint(jax.random.fold_in(key, 12), (), 0, groups)
    counts = jnp.where(jnp.arange(groups) == fullest, BCAP, counts)
    return counts.reshape(NX // CX, NY // CY).astype(jnp.int32)


def plant(entries, own_key, low, top_value):
    place = [jax.random.randint(jax.random.fold_in(own_key, axis), (), 0, length) for axis, length in enumerate(entries.shape)]
    main_axis = entries.shape.index(max(entries.shape))
    next_to = place[:main_axis] + [(place[main_axis] + 1) % entries.shape[main_axis]] + place[main_axis + 1:]
    return entries.at[tuple(place)].set(low).at[tuple(next_to)].set(top_value)


def steps_of(own_key, shape, cuts, least, top_value):
    def one(position, blocks):
        steps = jax.random.uniform(jax.random.fold_in(jax.random.fold_in(own_key, 6), position), (blocks,), jnp.float32, least / len(cuts), top_value / len(cuts))
        return jnp.repeat(jnp.exp(steps), shape[position] // blocks).reshape((-1,) + (1,) * (len(shape) - position - 1))

    factor_of = one(*cuts[0])
    for cut in cuts[1:]:
        factor_of = factor_of * one(*cut)
    return factor_of


def centred(rng, shape, width, most, shards=(), kind=jnp.bfloat16):
    level = steps_of(rng, shape, shards, -0.22, 0.18) if shards else 1.0
    entries = jax.random.normal(rng, shape, jnp.float32) * width * level
    return jnp.minimum(jnp.maximum(entries, -most), most).astype(kind)


def setup_inputs(seed: int = 0) -> dict:
    keys = jax.random.split(jax.random.key(seed), 9)
    velocity = centred(keys[0], (NX, NY, NZ), 1.0, 6.0, ((0, 64), (1, 16)), jnp.float32)
    cotangent = centred(keys[1], (NX, NY, NZ), 1.0, 6.0, ((0, 64), (1, 16)), jnp.float32)
    block_ids = draw_block_ids(jax.random.fold_in(keys[8], 71), 0)
    fluid_count = draw_fluid_count(jax.random.fold_in(keys[8], 71), 0)
    fluid_cells = plant((jax.random.randint(keys[4], (NX // CX, NY // CY, BCAP * 64), 0, 4) < 3).astype(jnp.int32), jax.random.fold_in(keys[4], 1), 0, 1)
    w_in = centred(keys[5], (CH, 7), 7 ** -0.5, 2.0)
    w_mid = centred(keys[6], (CH, CH), CH ** -0.5, 0.75)
    w_out = centred(keys[7], (1, CH), CH ** -0.5, 0.75)
    return {"velocity": velocity, "cotangent": cotangent, "block_ids": block_ids, "fluid_count": fluid_count, "fluid_cells": fluid_cells, "w_in": w_in, "w_mid": w_mid, "w_out": w_out}


viscosity = 0.1

def to_blocks(field):
    lead = field.shape[:-3]
    sizex, sizey, sizez = field.shape[-3:]
    count = len(lead)
    shaped = field.reshape(lead + (sizex // 4, 4, sizey // 4, 4, sizez // 4, 4))
    order = list(range(count)) + [count, count + 2, count + 4, count + 1, count + 3, count + 5]
    return shaped.transpose(order).reshape(lead + (sizex * sizey * sizez // 64, 64))

def from_blocks(blocks, sizex, sizey, sizez):
    lead = blocks.shape[:-2]
    count = len(lead)
    shaped = blocks.reshape(lead + (sizex // 4, sizey // 4, sizez // 4, 4, 4, 4))
    order = list(range(count)) + [count, count + 3, count + 1, count + 4, count + 2, count + 5]
    return shaped.transpose(order).reshape(lead + (sizex, sizey, sizez))

def closure_tile(padded, cotile, ids, count, fluid, w_in, w_mid, w_out):
    sizex = padded.shape[0] - 2
    sizey = padded.shape[1] - 2
    sizez = padded.shape[2]
    slots = ids.shape[0]
    nblocks = sizex * sizey * sizez // 64
    center = padded[1:-1, 1:-1]
    stencil = jnp.stack([center, padded[2:, 1:-1], padded[:-2, 1:-1], padded[1:-1, 2:], padded[1:-1, :-2], jnp.roll(center, -1, 2), jnp.roll(center, 1, 2)]).astype(jnp.bfloat16)
    chosen = jnp.take(to_blocks(stencil), ids, axis=1).reshape(7, slots * 64)
    live = (jnp.arange(slots) < count).astype(jnp.float32)
    weight = (fluid.reshape(slots, 64).astype(jnp.float32) * live[:, None]).reshape(slots * 64)
    h1 = jnp.tanh(jnp.dot(w_in, chosen, preferred_element_type=jnp.float32)).astype(jnp.bfloat16)
    h2 = jnp.tanh(jnp.dot(w_mid, h1, preferred_element_type=jnp.float32)).astype(jnp.bfloat16)
    closure = jnp.dot(w_out, h2, preferred_element_type=jnp.float32)[0] * weight
    corr_blocks = jnp.zeros((nblocks, 64), jnp.float32).at[ids].add(closure.reshape(slots, 64))
    corr = from_blocks(corr_blocks, sizex, sizey, sizez)
    cot_sel = jnp.take(to_blocks(cotile), ids, axis=0).reshape(slots * 64)
    dcl = (cot_sel * weight).astype(jnp.bfloat16)
    h2f = h2.astype(jnp.float32)
    h1f = h1.astype(jnp.float32)
    dh2 = jnp.dot(w_out.T, dcl[None, :], preferred_element_type=jnp.float32)
    da2 = (dh2 * (1.0 - h2f * h2f)).astype(jnp.bfloat16)
    dh1 = jnp.dot(w_mid.T, da2, preferred_element_type=jnp.float32)
    da1 = (dh1 * (1.0 - h1f * h1f)).astype(jnp.bfloat16)
    dfeat = jnp.dot(w_in.T, da1, preferred_element_type=jnp.float32)
    dims = (((1,), (1,)), ((), ()))
    gin = lax.dot_general(da1, chosen, dims, preferred_element_type=jnp.float32)
    gmid = lax.dot_general(da2, h1, dims, preferred_element_type=jnp.float32)
    gout = lax.dot_general(dcl[None, :], h2, dims, preferred_element_type=jnp.float32)
    dense = jnp.zeros((7, nblocks, 64), jnp.float32).at[:, ids].add(dfeat.reshape(7, slots, 64))
    dense = from_blocks(dense, sizex, sizey, sizez)
    local = dense[0] + jnp.roll(dense[5], 1, 2) + jnp.roll(dense[6], -1, 2)
    return (corr, local, dense[1:5], gin, gmid, gout)

def laplace(field):
    total = jnp.roll(field, -1, 0) + jnp.roll(field, 1, 0) + jnp.roll(field, -1, 1)
    total = total + jnp.roll(field, 1, 1) + jnp.roll(field, -1, 2) + jnp.roll(field, 1, 2)
    return total - 6.0 * field

def untile(tiles):
    return tiles.reshape(N_GX, N_GY, CX, CY, NZ).transpose(0, 2, 1, 3, 4).reshape(NX, NY, NZ)

def reference(velocity, cotangent, block_ids, fluid_count, fluid_cells, w_in, w_mid, w_out):
    wrapped = jnp.pad(velocity, ((1, 1), (1, 1), (0, 0)), mode='wrap')

    def one_tile(index):
        row = index // N_GY
        col = index % N_GY
        zero = jnp.zeros((), jnp.int32)
        padded = lax.dynamic_slice(wrapped, (row * CX, col * CY, zero), (CX + 2, CY + 2, NZ))
        cotile = lax.dynamic_slice(cotangent, (row * CX, col * CY, zero), (CX, CY, NZ))
        return closure_tile(padded, cotile, block_ids[row, col], fluid_count[row, col], fluid_cells[row, col], w_in, w_mid, w_out)
    corr, local, side, gin, gmid, gout = lax.map(one_tile, jnp.arange(N_GX * N_GY, dtype=jnp.int32))
    new_field = velocity + viscosity * laplace(velocity) + untile(corr)
    grad_field = cotangent + viscosity * laplace(cotangent) + untile(local)
    grad_field = grad_field + jnp.roll(untile(side[:, 0]), 1, 0) + jnp.roll(untile(side[:, 1]), -1, 0)
    grad_field = grad_field + jnp.roll(untile(side[:, 2]), 1, 1) + jnp.roll(untile(side[:, 3]), -1, 1)
    scale = 1.0 / jnp.sqrt(jnp.float32(N_GX * N_GY * BCAP * 64))
    return (new_field, grad_field, lax.optimization_barrier(jnp.sum(gin, 0)) * scale, lax.optimization_barrier(jnp.sum(gmid, 0)) * scale, lax.optimization_barrier(jnp.sum(gout, 0)) * scale)
```

```python
import jax
import jax.numpy as jnp
from jax import lax
from jax.sharding import PartitionSpec as P

viscosity = 0.1

GROUP_BITS = (("gx", 1), ("gy", 1))


def shift_from(face, axis, step):
    count = lax.axis_size(axis)
    return lax.ppermute(face, axis, [(i, (i + step) % count) for i in range(count)])


def group_sum(x, axis, lo, bits):
    count = lax.axis_size(axis)
    parts = [x]
    for m in range(1, 1 << bits):
        mask = m << lo
        parts.append(lax.ppermute(x, axis, [(i, i ^ mask) for i in range(count)]))
    while len(parts) > 1:
        parts = [parts[2 * k] + parts[2 * k + 1] for k in range(len(parts) // 2)]
    return parts[0]


def all_sum(x):
    for axis, chunk in GROUP_BITS:
        bits = lax.axis_size(axis).bit_length() - 1
        lo = 0
        while lo < bits:
            step = min(chunk, bits - lo)
            x = group_sum(x, axis, lo, step)
            lo += step
    return x


def from_blocks(blocks, sizex, sizey, sizez):
    lead = blocks.shape[:-2]
    count = len(lead)
    shaped = blocks.reshape(lead + (sizex // 4, sizey // 4, sizez // 4, 4, 4, 4))
    order = list(range(count)) + [count, count + 3, count + 1, count + 4, count + 2, count + 5]
    return shaped.transpose(order).reshape(lead + (sizex, sizey, sizez))


def padded_of(center, xlo, xhi, ylo, yhi):
    sizez = center.shape[-1]
    corner = jnp.zeros(center.shape[:-3] + (1, 1, sizez), center.dtype)
    mid = jnp.concatenate([ylo[..., :, None, :], center, yhi[..., :, None, :]], axis=-2)
    top = jnp.concatenate([corner, xlo[..., None, :, :], corner], axis=-2)
    bot = jnp.concatenate([corner, xhi[..., None, :, :], corner], axis=-2)
    return jnp.concatenate([top, mid, bot], axis=-3)


def padded_laplace(padded):
    center = padded[1:-1, 1:-1]
    total = padded[2:, 1:-1] + padded[:-2, 1:-1] + padded[1:-1, 2:] + padded[1:-1, :-2]
    total = total + jnp.roll(center, -1, 2) + jnp.roll(center, 1, 2)
    return total - 6.0 * center


def body(velocity, cotangent, block_ids, fluid_count, fluid_cells, w_in, w_mid, w_out):
    sizex, sizey, sizez = velocity.shape
    slots = block_ids.shape[2]
    nblocks = sizex * sizey * sizez // 64
    cells = sizex * sizey * sizez

    both = jnp.stack([velocity, cotangent])
    xlo = shift_from(both[:, -1], "gx", 1)
    xhi = shift_from(both[:, 0], "gx", -1)
    ylo = shift_from(both[:, :, -1], "gy", 1)
    yhi = shift_from(both[:, :, 0], "gy", -1)
    padded = padded_of(velocity, xlo[0], xhi[0], ylo[0], yhi[0])
    cot_pad = padded_of(cotangent, xlo[1], xhi[1], ylo[1], yhi[1])

    ids = block_ids.reshape(slots)
    live = (jnp.arange(slots) < fluid_count[0, 0]).astype(jnp.bfloat16)
    slot_w = fluid_cells.reshape(slots, 64).astype(jnp.bfloat16) * live[:, None]
    onehot = (ids[:, None] == jnp.arange(nblocks)[None, :]).astype(jnp.bfloat16)
    block_w = lax.dot_general(onehot, slot_w, (((0,), (0,)), ((), ())), preferred_element_type=jnp.float32)
    weight = from_blocks(block_w, sizex, sizey, sizez).reshape(cells)

    center = padded[1:-1, 1:-1]
    chosen = jnp.stack(
        [
            center,
            padded[2:, 1:-1],
            padded[:-2, 1:-1],
            padded[1:-1, 2:],
            padded[1:-1, :-2],
            jnp.roll(center, -1, 2),
            jnp.roll(center, 1, 2),
        ]
    ).astype(jnp.bfloat16).reshape(7, cells)
    h1 = jnp.tanh(jnp.dot(w_in, chosen, preferred_element_type=jnp.float32)).astype(jnp.bfloat16)
    h2 = jnp.tanh(jnp.dot(w_mid, h1, preferred_element_type=jnp.float32)).astype(jnp.bfloat16)
    corr = jnp.dot(w_out, h2, preferred_element_type=jnp.float32)[0] * weight
    dcl = (cotangent.reshape(cells) * weight).astype(jnp.bfloat16)
    h2f = h2.astype(jnp.float32)
    h1f = h1.astype(jnp.float32)
    dh2 = jnp.dot(w_out.T, dcl[None, :], preferred_element_type=jnp.float32)
    da2 = (dh2 * (1.0 - h2f * h2f)).astype(jnp.bfloat16)
    dh1 = jnp.dot(w_mid.T, da2, preferred_element_type=jnp.float32)
    da1 = (dh1 * (1.0 - h1f * h1f)).astype(jnp.bfloat16)
    dfeat = jnp.dot(w_in.T, da1, preferred_element_type=jnp.float32).reshape(7, sizex, sizey, sizez)
    dims = (((1,), (1,)), ((), ()))
    gin = lax.dot_general(da1, chosen, dims, preferred_element_type=jnp.float32)
    gmid = lax.dot_general(da2, h1, dims, preferred_element_type=jnp.float32)
    gout = lax.dot_general(dcl[None, :], h2, dims, preferred_element_type=jnp.float32)

    new_field = velocity + viscosity * padded_laplace(padded) + corr.reshape(sizex, sizey, sizez)

    from_xlo = shift_from(dfeat[1, -1], "gx", 1)
    from_xhi = shift_from(dfeat[2, 0], "gx", -1)
    from_ylo = shift_from(dfeat[3, :, -1], "gy", 1)
    from_yhi = shift_from(dfeat[4, :, 0], "gy", -1)
    side1 = jnp.concatenate([from_xlo[None], dfeat[1, :-1]], axis=0)
    side2 = jnp.concatenate([dfeat[2, 1:], from_xhi[None]], axis=0)
    side3 = jnp.concatenate([from_ylo[:, None], dfeat[3, :, :-1]], axis=1)
    side4 = jnp.concatenate([dfeat[4, :, 1:], from_yhi[:, None]], axis=1)
    local = dfeat[0] + jnp.roll(dfeat[5], 1, 2) + jnp.roll(dfeat[6], -1, 2)
    grad_field = cotangent + viscosity * padded_laplace(cot_pad) + local + (side1 + side2 + side3 + side4)

    flat = jnp.concatenate([gin.reshape(-1), gmid.reshape(-1), gout.reshape(-1)])
    total = all_sum(flat)
    scale = 1.0 / jnp.sqrt(jnp.float32(lax.axis_size("gx") * lax.axis_size("gy") * slots * 64))
    total = total * scale
    width = gmid.shape[0]
    grad_in = total[: width * 7].reshape(width, 7)
    grad_mid = total[width * 7 : width * 7 + width * width].reshape(width, width)
    grad_out = total[width * 7 + width * width :].reshape(1, width)
    return (new_field, grad_field, grad_in, grad_mid, grad_out)


def solution(mesh):
    in_specs = (
        P("gx", "gy", None),
        P("gx", "gy", None),
        P("gx", "gy", None),
        P("gx", "gy"),
        P("gx", "gy", None),
        P(),
        P(),
        P(),
    )
    out_specs = (P("gx", "gy", None), P("gx", "gy", None), P(), P(), P())
    return jax.shard_map(body, mesh=mesh, in_specs=in_specs, out_specs=out_specs, check_vma=False)
```

```python
import jax
import jax.numpy as jnp
from jax import lax
from jax.sharding import PartitionSpec as P

viscosity = 0.1


def shift_from(face, axis, step):
    count = lax.axis_size(axis)
    return lax.ppermute(face, axis, [(i, (i + step) % count) for i in range(count)])


def group_sum(x, axis, lo, bits):
    count = lax.axis_size(axis)
    parts = [x]
    for m in range(1, 1 << bits):
        mask = m << lo
        parts.append(lax.ppermute(x, axis, [(i, i ^ mask) for i in range(count)]))
    while len(parts) > 1:
        parts = [parts[2 * k] + parts[2 * k + 1] for k in range(len(parts) // 2)]
    return parts[0]


def torus_rounds():
    def decode(i):
        gx, gy = divmod(i, 16)
        return {"core": gx % 2, "x": (gx // 2) % 8, "y": (gy % 2) * 4 + gx // 16, "z": gy // 2}

    def encode(c):
        return ((c["y"] % 4) * 16 + c["x"] * 2 + c["core"]) * 16 + c["z"] * 2 + c["y"] // 4

    rounds = []
    for ring, size in (("core", 2), ("x", 8), ("y", 8), ("z", 8)):
        steps = [(lambda v, b=b: v ^ b) for b in (1, 2, 4, 8) if 2 * b < size]
        steps.append(lambda v, size=size: size - 1 - v)
        for step in steps:
            pairs = []
            for i in range(1024):
                c = decode(i)
                c[ring] = step(c[ring])
                pairs.append((i, encode(c)))
            rounds.append(pairs)
    return rounds


def all_sum(x):
    if (lax.axis_size("gx"), lax.axis_size("gy")) == (64, 16):
        for pairs in torus_rounds():
            x = x + lax.ppermute(x, ("gx", "gy"), pairs)
        return x
    for axis in ("gx", "gy"):
        for lo in range(lax.axis_size(axis).bit_length() - 1):
            x = group_sum(x, axis, lo, 1)
    return x


def from_blocks(blocks, sizex, sizey, sizez):
    lead = blocks.shape[:-2]
    count = len(lead)
    shaped = blocks.reshape(lead + (sizex // 4, sizey // 4, sizez // 4, 4, 4, 4))
    order = list(range(count)) + [count, count + 3, count + 1, count + 4, count + 2, count + 5]
    return shaped.transpose(order).reshape(lead + (sizex, sizey, sizez))


def padded_of(center, xlo, xhi, ylo, yhi):
    sizez = center.shape[-1]
    corner = jnp.zeros(center.shape[:-3] + (1, 1, sizez), center.dtype)
    mid = jnp.concatenate([ylo[..., :, None, :], center, yhi[..., :, None, :]], axis=-2)
    top = jnp.concatenate([corner, xlo[..., None, :, :], corner], axis=-2)
    bot = jnp.concatenate([corner, xhi[..., None, :, :], corner], axis=-2)
    return jnp.concatenate([top, mid, bot], axis=-3)


def padded_laplace(padded):
    center = padded[1:-1, 1:-1]
    total = padded[2:, 1:-1] + padded[:-2, 1:-1] + padded[1:-1, 2:] + padded[1:-1, :-2]
    total = total + jnp.roll(center, -1, 2) + jnp.roll(center, 1, 2)
    return total - 6.0 * center


def body(velocity, cotangent, block_ids, fluid_count, fluid_cells, w_in, w_mid, w_out):
    sizex, sizey, sizez = velocity.shape
    slots = block_ids.shape[2]
    nblocks = sizex * sizey * sizez // 64
    cells = sizex * sizey * sizez

    both = jnp.stack([velocity, cotangent])
    xlo = shift_from(both[:, -1], "gx", 1)
    xhi = shift_from(both[:, 0], "gx", -1)
    ylo = shift_from(both[:, :, -1], "gy", 1)
    yhi = shift_from(both[:, :, 0], "gy", -1)
    padded = padded_of(velocity, xlo[0], xhi[0], ylo[0], yhi[0])
    cot_pad = padded_of(cotangent, xlo[1], xhi[1], ylo[1], yhi[1])

    ids = block_ids.reshape(slots)
    live = (jnp.arange(slots) < fluid_count[0, 0]).astype(jnp.bfloat16)
    slot_w = fluid_cells.reshape(slots, 64).astype(jnp.bfloat16) * live[:, None]
    onehot = (ids[:, None] == jnp.arange(nblocks)[None, :]).astype(jnp.bfloat16)
    block_w = lax.dot_general(onehot, slot_w, (((0,), (0,)), ((), ())), preferred_element_type=jnp.float32)
    weight = from_blocks(block_w, sizex, sizey, sizez).reshape(cells)

    center = padded[1:-1, 1:-1]
    chosen = jnp.stack(
        [
            center,
            padded[2:, 1:-1],
            padded[:-2, 1:-1],
            padded[1:-1, 2:],
            padded[1:-1, :-2],
            jnp.roll(center, -1, 2),
            jnp.roll(center, 1, 2),
        ]
    ).astype(jnp.bfloat16).reshape(7, cells)
    h1 = jnp.tanh(jnp.dot(w_in, chosen, preferred_element_type=jnp.float32)).astype(jnp.bfloat16)
    h2 = jnp.tanh(jnp.dot(w_mid, h1, preferred_element_type=jnp.float32)).astype(jnp.bfloat16)
    corr = jnp.dot(w_out, h2, preferred_element_type=jnp.float32)[0] * weight
    dcl = (cotangent.reshape(cells) * weight).astype(jnp.bfloat16)
    h2f = h2.astype(jnp.float32)
    h1f = h1.astype(jnp.float32)
    dh2 = jnp.dot(w_out.T, dcl[None, :], preferred_element_type=jnp.float32)
    da2 = (dh2 * (1.0 - h2f * h2f)).astype(jnp.bfloat16)
    dh1 = jnp.dot(w_mid.T, da2, preferred_element_type=jnp.float32)
    da1 = (dh1 * (1.0 - h1f * h1f)).astype(jnp.bfloat16)
    dfeat = jnp.dot(w_in.T, da1, preferred_element_type=jnp.float32).reshape(7, sizex, sizey, sizez)
    dims = (((1,), (1,)), ((), ()))
    gin = lax.dot_general(da1, chosen, dims, preferred_element_type=jnp.float32)
    gmid = lax.dot_general(da2, h1, dims, preferred_element_type=jnp.float32)
    gout = lax.dot_general(dcl[None, :], h2, dims, preferred_element_type=jnp.float32)

    new_field = velocity + viscosity * padded_laplace(padded) + corr.reshape(sizex, sizey, sizez)

    from_xlo = shift_from(dfeat[1, -1], "gx", 1)
    from_xhi = shift_from(dfeat[2, 0], "gx", -1)
    from_ylo = shift_from(dfeat[3, :, -1], "gy", 1)
    from_yhi = shift_from(dfeat[4, :, 0], "gy", -1)

    flat = jnp.concatenate([gin.reshape(-1), gmid.reshape(-1), gout.reshape(-1)])
    flat, from_xlo, from_xhi, from_ylo, from_yhi = lax.optimization_barrier((flat, from_xlo, from_xhi, from_ylo, from_yhi))
    total = all_sum(flat)
    side1 = jnp.concatenate([from_xlo[None], dfeat[1, :-1]], axis=0)
    side2 = jnp.concatenate([dfeat[2, 1:], from_xhi[None]], axis=0)
    side3 = jnp.concatenate([from_ylo[:, None], dfeat[3, :, :-1]], axis=1)
    side4 = jnp.concatenate([dfeat[4, :, 1:], from_yhi[:, None]], axis=1)
    local = dfeat[0] + jnp.roll(dfeat[5], 1, 2) + jnp.roll(dfeat[6], -1, 2)
    grad_field = cotangent + viscosity * padded_laplace(cot_pad) + local + (side1 + side2 + side3 + side4)

    scale = 1.0 / jnp.sqrt(jnp.float32(lax.axis_size("gx") * lax.axis_size("gy") * slots * 64))
    total = total * scale
    width = gmid.shape[0]
    grad_in = total[: width * 7].reshape(width, 7)
    grad_mid = total[width * 7 : width * 7 + width * width].reshape(width, width)
    grad_out = total[width * 7 + width * width :].reshape(1, width)
    return (new_field, grad_field, grad_in, grad_mid, grad_out)


def solution(mesh):
    in_specs = (
        P("gx", "gy", None),
        P("gx", "gy", None),
        P("gx", "gy", None),
        P("gx", "gy"),
        P("gx", "gy", None),
        P(),
        P(),
        P(),
    )
    out_specs = (P("gx", "gy", None), P("gx", "gy", None), P(), P(), P())
    return jax.shard_map(body, mesh=mesh, in_specs=in_specs, out_specs=out_specs, check_vma=False)
```

```python
import jax
import jax.numpy as jnp
from jax import lax
from jax.sharding import PartitionSpec as P

viscosity = 0.1


def shift_from(face, axis, step):
    count = lax.axis_size(axis)
    return lax.ppermute(face, axis, [(i, (i + step) % count) for i in range(count)])


def group_sum(x, axis, lo, bits):
    count = lax.axis_size(axis)
    parts = [x]
    for m in range(1, 1 << bits):
        mask = m << lo
        parts.append(lax.ppermute(x, axis, [(i, i ^ mask) for i in range(count)]))
    while len(parts) > 1:
        parts = [parts[2 * k] + parts[2 * k + 1] for k in range(len(parts) // 2)]
    return parts[0]


def torus_rounds():
    def decode(i):
        gx, gy = divmod(i, 16)
        return {"core": gx % 2, "x": (gx // 2) % 8, "y": (gy % 2) * 4 + gx // 16, "z": gy // 2}

    def encode(c):
        return ((c["y"] % 4) * 16 + c["x"] * 2 + c["core"]) * 16 + c["z"] * 2 + c["y"] // 4

    rounds = []
    for ring, size in (("core", 2), ("x", 8), ("y", 8), ("z", 8)):
        steps = [(lambda v, b=b: v ^ b) for b in (1, 2, 4, 8) if 2 * b < size]
        steps.append(lambda v, size=size: size - 1 - v)
        for step in steps:
            pairs = []
            for i in range(1024):
                c = decode(i)
                c[ring] = step(c[ring])
                pairs.append((i, encode(c)))
            rounds.append(pairs)
    return rounds


def all_sum(x):
    if (lax.axis_size("gx"), lax.axis_size("gy")) == (64, 16):
        for pairs in torus_rounds():
            x = x + lax.ppermute(x, ("gx", "gy"), pairs)
        return x
    for axis in ("gx", "gy"):
        for lo in range(lax.axis_size(axis).bit_length() - 1):
            x = group_sum(x, axis, lo, 1)
    return x


def from_blocks(blocks, sizex, sizey, sizez):
    lead = blocks.shape[:-2]
    count = len(lead)
    shaped = blocks.reshape(lead + (sizex // 4, sizey // 4, sizez // 4, 4, 4, 4))
    order = list(range(count)) + [count, count + 3, count + 1, count + 4, count + 2, count + 5]
    return shaped.transpose(order).reshape(lead + (sizex, sizey, sizez))


def padded_of(center, xlo, xhi, ylo, yhi):
    sizez = center.shape[-1]
    corner = jnp.zeros(center.shape[:-3] + (1, 1, sizez), center.dtype)
    mid = jnp.concatenate([ylo[..., :, None, :], center, yhi[..., :, None, :]], axis=-2)
    top = jnp.concatenate([corner, xlo[..., None, :, :], corner], axis=-2)
    bot = jnp.concatenate([corner, xhi[..., None, :, :], corner], axis=-2)
    return jnp.concatenate([top, mid, bot], axis=-3)


def padded_laplace(padded):
    center = padded[1:-1, 1:-1]
    total = padded[2:, 1:-1] + padded[:-2, 1:-1] + padded[1:-1, 2:] + padded[1:-1, :-2]
    total = total + jnp.roll(center, -1, 2) + jnp.roll(center, 1, 2)
    return total - 6.0 * center


def body(velocity, cotangent, block_ids, fluid_count, fluid_cells, w_in, w_mid, w_out):
    sizex, sizey, sizez = velocity.shape
    slots = block_ids.shape[2]
    nblocks = sizex * sizey * sizez // 64
    cells = sizex * sizey * sizez

    both = jnp.stack([velocity, cotangent])
    xlo = shift_from(both[:, -1], "gx", 1)
    xhi = shift_from(both[:, 0], "gx", -1)
    ylo = shift_from(both[:, :, -1], "gy", 1)
    yhi = shift_from(both[:, :, 0], "gy", -1)
    padded = padded_of(velocity, xlo[0], xhi[0], ylo[0], yhi[0])
    cot_pad = padded_of(cotangent, xlo[1], xhi[1], ylo[1], yhi[1])

    ids = block_ids.reshape(slots)
    live = (jnp.arange(slots) < fluid_count[0, 0]).astype(jnp.bfloat16)
    slot_w = fluid_cells.reshape(slots, 64).astype(jnp.bfloat16) * live[:, None]
    onehot = (ids[:, None] == jnp.arange(nblocks)[None, :]).astype(jnp.bfloat16)
    block_w = lax.dot_general(onehot, slot_w, (((0,), (0,)), ((), ())), preferred_element_type=jnp.float32)
    weight = from_blocks(block_w, sizex, sizey, sizez).reshape(cells)

    center = padded[1:-1, 1:-1]
    chosen = jnp.stack(
        [
            center,
            padded[2:, 1:-1],
            padded[:-2, 1:-1],
            padded[1:-1, 2:],
            padded[1:-1, :-2],
            jnp.roll(center, -1, 2),
            jnp.roll(center, 1, 2),
        ]
    ).astype(jnp.bfloat16).reshape(7, cells)
    h1 = jnp.tanh(jnp.dot(w_in, chosen, preferred_element_type=jnp.float32)).astype(jnp.bfloat16)
    h2 = jnp.tanh(jnp.dot(w_mid, h1, preferred_element_type=jnp.float32)).astype(jnp.bfloat16)
    corr = jnp.dot(w_out, h2, preferred_element_type=jnp.float32)[0] * weight
    dcl = (cotangent.reshape(cells) * weight).astype(jnp.bfloat16)
    h2f = h2.astype(jnp.float32)
    h1f = h1.astype(jnp.float32)
    dh2 = jnp.dot(w_out.T, dcl[None, :], preferred_element_type=jnp.float32)
    da2 = (dh2 * (1.0 - h2f * h2f)).astype(jnp.bfloat16)
    dh1 = jnp.dot(w_mid.T, da2, preferred_element_type=jnp.float32)
    da1 = (dh1 * (1.0 - h1f * h1f)).astype(jnp.bfloat16)
    dfeat = jnp.dot(w_in.T, da1, preferred_element_type=jnp.float32).reshape(7, sizex, sizey, sizez)
    dims = (((1,), (1,)), ((), ()))
    gin = lax.dot_general(da1, chosen, dims, preferred_element_type=jnp.float32)
    gmid = lax.dot_general(da2, h1, dims, preferred_element_type=jnp.float32)
    gout = lax.dot_general(dcl[None, :], h2, dims, preferred_element_type=jnp.float32)

    new_field = velocity + viscosity * padded_laplace(padded) + corr.reshape(sizex, sizey, sizez)

    from_xlo = shift_from(dfeat[1, -1], "gx", 1)
    from_xhi = shift_from(dfeat[2, 0], "gx", -1)
    from_ylo = shift_from(dfeat[3, :, -1], "gy", 1)
    from_yhi = shift_from(dfeat[4, :, 0], "gy", -1)

    flat = jnp.concatenate([gin.reshape(-1), gmid.reshape(-1), gout.reshape(-1)])
    padded_flat = jnp.pad(flat, (0, max(0, 16384 - flat.shape[0])))
    total = lax.psum(padded_flat, ("gx", "gy"))[: flat.shape[0]]
    side1 = jnp.concatenate([from_xlo[None], dfeat[1, :-1]], axis=0)
    side2 = jnp.concatenate([dfeat[2, 1:], from_xhi[None]], axis=0)
    side3 = jnp.concatenate([from_ylo[:, None], dfeat[3, :, :-1]], axis=1)
    side4 = jnp.concatenate([dfeat[4, :, 1:], from_yhi[:, None]], axis=1)
    local = dfeat[0] + jnp.roll(dfeat[5], 1, 2) + jnp.roll(dfeat[6], -1, 2)
    grad_field = cotangent + viscosity * padded_laplace(cot_pad) + local + (side1 + side2 + side3 + side4)

    scale = 1.0 / jnp.sqrt(jnp.float32(lax.axis_size("gx") * lax.axis_size("gy") * slots * 64))
    total = total * scale
    width = gmid.shape[0]
    grad_in = total[: width * 7].reshape(width, 7)
    grad_mid = total[width * 7 : width * 7 + width * width].reshape(width, width)
    grad_out = total[width * 7 + width * width :].reshape(1, width)
    return (new_field, grad_field, grad_in, grad_mid, grad_out)


def solution(mesh):
    in_specs = (
        P("gx", "gy", None),
        P("gx", "gy", None),
        P("gx", "gy", None),
        P("gx", "gy"),
        P("gx", "gy", None),
        P(),
        P(),
        P(),
    )
    out_specs = (P("gx", "gy", None), P("gx", "gy", None), P(), P(), P())
    return jax.shard_map(body, mesh=mesh, in_specs=in_specs, out_specs=out_specs, check_vma=False)
```

```python
import jax
import jax.numpy as jnp
from jax import lax
from jax.sharding import PartitionSpec as P

viscosity = 0.1


def shift_from(face, axis, step):
    count = lax.axis_size(axis)
    return lax.ppermute(face, axis, [(i, (i + step) % count) for i in range(count)])


def reduce_rounds(nx, ny):
    if (nx, ny) == (64, 16):
        def decode(i):
            gx, gy = divmod(i, 16)
            return {"core": gx % 2, "x": (gx // 2) % 8, "y": (gy % 2) * 4 + gx // 16, "z": gy // 2}

        def encode(c):
            return ((c["y"] % 4) * 16 + c["x"] * 2 + c["core"]) * 16 + c["z"] * 2 + c["y"] // 4

        plan = [
            ("core", lambda v: v ^ 1, "gx"),
            ("y", lambda v: v ^ 4, "gy"),
            ("x", lambda v: v ^ 1, None),
            ("x", lambda v: v ^ 2, None),
            ("x", lambda v: 7 - v, None),
            ("y", lambda v: v ^ 1, None),
            ("y", lambda v: v ^ 2, None),
            ("z", lambda v: v ^ 1, None),
            ("z", lambda v: v ^ 2, None),
            ("z", lambda v: 7 - v, None),
        ]
        rounds = []
        for ring, step, tag in plan:
            pairs = []
            for i in range(nx * ny):
                c = decode(i)
                c[ring] = step(c[ring])
                pairs.append((i, encode(c)))
            rounds.append((pairs, tag))
        return rounds
    rounds = []
    for size, stride, tag in ((nx, ny, "gx"), (ny, 1, "gy")):
        for bit in range(size.bit_length() - 1):
            pairs = []
            for i in range(nx * ny):
                index = (i // stride) % size
                pairs.append((i, i + ((index ^ (1 << bit)) - index) * stride))
            rounds.append((pairs, tag if bit == 0 else None))
    return rounds


def from_blocks(blocks, sizex, sizey, sizez):
    lead = blocks.shape[:-2]
    count = len(lead)
    shaped = blocks.reshape(lead + (sizex // 4, sizey // 4, sizez // 4, 4, 4, 4))
    order = list(range(count)) + [count, count + 3, count + 1, count + 4, count + 2, count + 5]
    return shaped.transpose(order).reshape(lead + (sizex, sizey, sizez))


def padded_of(center, xlo, xhi, ylo, yhi):
    sizez = center.shape[-1]
    corner = jnp.zeros(center.shape[:-3] + (1, 1, sizez), center.dtype)
    mid = jnp.concatenate([ylo[..., :, None, :], center, yhi[..., :, None, :]], axis=-2)
    top = jnp.concatenate([corner, xlo[..., None, :, :], corner], axis=-2)
    bot = jnp.concatenate([corner, xhi[..., None, :, :], corner], axis=-2)
    return jnp.concatenate([top, mid, bot], axis=-3)


def padded_laplace(padded):
    center = padded[1:-1, 1:-1]
    total = padded[2:, 1:-1] + padded[:-2, 1:-1] + padded[1:-1, 2:] + padded[1:-1, :-2]
    total = total + jnp.roll(center, -1, 2) + jnp.roll(center, 1, 2)
    return total - 6.0 * center


def body(velocity, cotangent, block_ids, fluid_count, fluid_cells, w_in, w_mid, w_out):
    sizex, sizey, sizez = velocity.shape
    slots = block_ids.shape[2]
    nblocks = sizex * sizey * sizez // 64
    cells = sizex * sizey * sizez

    both = jnp.stack([velocity, cotangent])
    xlo = shift_from(both[:, -1], "gx", 1)
    xhi = shift_from(both[:, 0], "gx", -1)
    ylo = shift_from(both[:, :, -1], "gy", 1)
    yhi = shift_from(both[:, :, 0], "gy", -1)
    padded = padded_of(velocity, xlo[0], xhi[0], ylo[0], yhi[0])
    cot_pad = padded_of(cotangent, xlo[1], xhi[1], ylo[1], yhi[1])

    ids = block_ids.reshape(slots)
    live = (jnp.arange(slots) < fluid_count[0, 0]).astype(jnp.bfloat16)
    slot_w = fluid_cells.reshape(slots, 64).astype(jnp.bfloat16) * live[:, None]
    onehot = (ids[:, None] == jnp.arange(nblocks)[None, :]).astype(jnp.bfloat16)
    block_w = lax.dot_general(onehot, slot_w, (((0,), (0,)), ((), ())), preferred_element_type=jnp.float32)
    weight = from_blocks(block_w, sizex, sizey, sizez).reshape(cells)

    center = padded[1:-1, 1:-1]
    chosen = jnp.stack(
        [
            center,
            padded[2:, 1:-1],
            padded[:-2, 1:-1],
            padded[1:-1, 2:],
            padded[1:-1, :-2],
            jnp.roll(center, -1, 2),
            jnp.roll(center, 1, 2),
        ]
    ).astype(jnp.bfloat16).reshape(7, cells)
    h1 = jnp.tanh(jnp.dot(w_in, chosen, preferred_element_type=jnp.float32)).astype(jnp.bfloat16)
    h2 = jnp.tanh(jnp.dot(w_mid, h1, preferred_element_type=jnp.float32)).astype(jnp.bfloat16)
    corr = jnp.dot(w_out, h2, preferred_element_type=jnp.float32)[0] * weight
    dcl = (cotangent.reshape(cells) * weight).astype(jnp.bfloat16)
    h2f = h2.astype(jnp.float32)
    h1f = h1.astype(jnp.float32)
    dh2 = jnp.dot(w_out.T, dcl[None, :], preferred_element_type=jnp.float32)
    da2 = (dh2 * (1.0 - h2f * h2f)).astype(jnp.bfloat16)
    dh1 = jnp.dot(w_mid.T, da2, preferred_element_type=jnp.float32)
    da1 = (dh1 * (1.0 - h1f * h1f)).astype(jnp.bfloat16)
    dfeat = jnp.dot(w_in.T, da1, preferred_element_type=jnp.float32).reshape(7, sizex, sizey, sizez)
    dims = (((1,), (1,)), ((), ()))
    gmid = lax.dot_general(da2, h1, dims, preferred_element_type=jnp.float32)
    gout = lax.dot_general(dcl[None, :], h2, dims, preferred_element_type=jnp.float32)

    new_field = velocity + viscosity * padded_laplace(padded) + corr.reshape(sizex, sizey, sizez)

    nx = lax.axis_size("gx")
    ny = lax.axis_size("gy")
    xodd = lax.axis_index("gx") % 2 == 1
    yodd = lax.axis_index("gy") % 2 == 1
    up_x, down_x = dfeat[1, -1], dfeat[2, 0]
    up_y, down_y = dfeat[3, :, -1], dfeat[4, :, 0]
    pair_face = {"gx": jnp.where(xodd, down_x, up_x), "gy": jnp.where(yodd, down_y, up_y)}
    other_x = lax.ppermute(
        jnp.where(xodd, up_x, down_x), "gx", [(i, (i + 1) % nx if i % 2 else (i - 1) % nx) for i in range(nx)]
    )
    other_y = lax.ppermute(
        jnp.where(yodd, up_y, down_y), "gy", [(i, (i + 1) % ny if i % 2 else (i - 1) % ny) for i in range(ny)]
    )

    gin_t = lax.dot_general(chosen, da1, dims, preferred_element_type=jnp.float32)
    grads = jnp.concatenate([gmid, gin_t, gout], axis=0)
    received = {}
    for pairs, tag in reduce_rounds(nx, ny):
        if tag is None:
            grads = grads + lax.ppermute(grads, ("gx", "gy"), pairs)
        else:
            rows = grads.shape[0]
            face = pair_face[tag]
            message = jnp.concatenate([grads, face.reshape(-1, grads.shape[1])], axis=0)
            got = lax.ppermute(message, ("gx", "gy"), pairs)
            received[tag] = got[rows:].reshape(face.shape)
            grads = grads + got[:rows]
    from_xlo = jnp.where(xodd, received["gx"], other_x)
    from_xhi = jnp.where(xodd, other_x, received["gx"])
    from_ylo = jnp.where(yodd, received["gy"], other_y)
    from_yhi = jnp.where(yodd, other_y, received["gy"])

    side1 = jnp.concatenate([from_xlo[None], dfeat[1, :-1]], axis=0)
    side2 = jnp.concatenate([dfeat[2, 1:], from_xhi[None]], axis=0)
    side3 = jnp.concatenate([from_ylo[:, None], dfeat[3, :, :-1]], axis=1)
    side4 = jnp.concatenate([dfeat[4, :, 1:], from_yhi[:, None]], axis=1)
    local = dfeat[0] + jnp.roll(dfeat[5], 1, 2) + jnp.roll(dfeat[6], -1, 2)
    grad_field = cotangent + viscosity * padded_laplace(cot_pad) + local + (side1 + side2 + side3 + side4)

    scale = 1.0 / jnp.sqrt(jnp.float32(nx * ny * slots * 64))
    total = grads * scale
    width = gmid.shape[0]
    grad_mid = total[:width]
    grad_in = total[width : width + 7].T
    grad_out = total[width + 7 :]
    return (new_field, grad_field, grad_in, grad_mid, grad_out)


def solution(mesh):
    in_specs = (
        P("gx", "gy", None),
        P("gx", "gy", None),
        P("gx", "gy", None),
        P("gx", "gy"),
        P("gx", "gy", None),
        P(),
        P(),
        P(),
    )
    out_specs = (P("gx", "gy", None), P("gx", "gy", None), P(), P(), P())
    return jax.shard_map(body, mesh=mesh, in_specs=in_specs, out_specs=out_specs, check_vma=False)
```

```python
import jax
import jax.numpy as jnp
from jax import lax
from jax.experimental import pallas as pl
from jax.experimental.pallas import tpu as pltpu
from jax.sharding import PartitionSpec as P

viscosity = 0.1


def shift_from(face, axis, step):
    count = lax.axis_size(axis)
    return lax.ppermute(face, axis, [(i, (i + step) % count) for i in range(count)])


def reduce_rounds(nx, ny):
    if (nx, ny) == (64, 16):
        def decode(i):
            gx, gy = divmod(i, 16)
            return {"core": gx % 2, "x": (gx // 2) % 8, "y": (gy % 2) * 4 + gx // 16, "z": gy // 2}

        def encode(c):
            return ((c["y"] % 4) * 16 + c["x"] * 2 + c["core"]) * 16 + c["z"] * 2 + c["y"] // 4

        plan = [
            ("core", lambda v: v ^ 1, "gx"),
            ("y", lambda v: v ^ 4, "gy"),
            ("x", lambda v: v ^ 1, None),
            ("x", lambda v: v ^ 2, None),
            ("x", lambda v: 7 - v, None),
            ("y", lambda v: v ^ 1, None),
            ("y", lambda v: v ^ 2, None),
            ("z", lambda v: v ^ 1, None),
            ("z", lambda v: v ^ 2, None),
            ("z", lambda v: 7 - v, None),
        ]
        rounds = []
        for ring, step, tag in plan:
            pairs = []
            for i in range(nx * ny):
                c = decode(i)
                c[ring] = step(c[ring])
                pairs.append((i, encode(c)))
            rounds.append((pairs, tag))
        return rounds
    rounds = []
    for size, stride, tag in ((nx, ny, "gx"), (ny, 1, "gy")):
        for bit in range(size.bit_length() - 1):
            pairs = []
            for i in range(nx * ny):
                index = (i // stride) % size
                pairs.append((i, i + ((index ^ (1 << bit)) - index) * stride))
            rounds.append((pairs, tag if bit == 0 else None))
    return rounds


def from_blocks(blocks, sizex, sizey, sizez):
    lead = blocks.shape[:-2]
    count = len(lead)
    shaped = blocks.reshape(lead + (sizex // 4, sizey // 4, sizez // 4, 4, 4, 4))
    order = list(range(count)) + [count, count + 3, count + 1, count + 4, count + 2, count + 5]
    return shaped.transpose(order).reshape(lead + (sizex, sizey, sizez))


def padded_of(center, xlo, xhi, ylo, yhi):
    sizez = center.shape[-1]
    corner = jnp.zeros(center.shape[:-3] + (1, 1, sizez), center.dtype)
    mid = jnp.concatenate([ylo[..., :, None, :], center, yhi[..., :, None, :]], axis=-2)
    top = jnp.concatenate([corner, xlo[..., None, :, :], corner], axis=-2)
    bot = jnp.concatenate([corner, xhi[..., None, :, :], corner], axis=-2)
    return jnp.concatenate([top, mid, bot], axis=-3)


def padded_laplace(padded, zup, zdown):
    center = padded[1:-1, 1:-1]
    total = padded[2:, 1:-1] + padded[:-2, 1:-1] + padded[1:-1, 2:] + padded[1:-1, :-2]
    total = total + zup + zdown
    return total - 6.0 * center


def z_neighbours_kernel(v_ref, c_ref, vup_ref, vdown_ref, cup_ref, cdown_ref):
    last = v_ref.shape[1] - 1
    v = v_ref[...]
    c = c_ref[...]
    vup_ref[...] = pltpu.roll(v, last, 1)
    vdown_ref[...] = pltpu.roll(v, 1, 1)
    cup_ref[...] = pltpu.roll(c, last, 1)
    cdown_ref[...] = pltpu.roll(c, 1, 1)


def z_neighbours(velocity, cotangent):
    shape = velocity.shape
    flat = (shape[0] * shape[1], shape[2])
    out = jax.ShapeDtypeStruct(flat, velocity.dtype)
    parts = pl.pallas_call(z_neighbours_kernel, out_shape=(out, out, out, out))(
        velocity.reshape(flat), cotangent.reshape(flat)
    )
    return [part.reshape(shape) for part in parts]


def body(velocity, cotangent, block_ids, fluid_count, fluid_cells, w_in, w_mid, w_out):
    sizex, sizey, sizez = velocity.shape
    slots = block_ids.shape[2]
    nblocks = sizex * sizey * sizez // 64
    cells = sizex * sizey * sizez

    xlo = shift_from(jnp.stack([velocity[-1], cotangent[-1]]), "gx", 1)
    xhi = shift_from(jnp.stack([velocity[0], cotangent[0]]), "gx", -1)
    ylo = shift_from(jnp.stack([velocity[:, -1], cotangent[:, -1]]), "gy", 1)
    yhi = shift_from(jnp.stack([velocity[:, 0], cotangent[:, 0]]), "gy", -1)
    vup, vdown, cup, cdown = z_neighbours(velocity, cotangent)
    padded = padded_of(velocity, xlo[0], xhi[0], ylo[0], yhi[0])
    cot_pad = padded_of(cotangent, xlo[1], xhi[1], ylo[1], yhi[1])

    ids = block_ids.reshape(slots)
    live = (jnp.arange(slots) < fluid_count[0, 0]).astype(jnp.bfloat16)
    slot_w = fluid_cells.reshape(slots, 64).astype(jnp.bfloat16) * live[:, None]
    onehot = (ids[:, None] == jnp.arange(nblocks)[None, :]).astype(jnp.bfloat16)
    block_w = lax.dot_general(onehot, slot_w, (((0,), (0,)), ((), ())), preferred_element_type=jnp.float32)
    weight = from_blocks(block_w, sizex, sizey, sizez).reshape(cells)

    center = padded[1:-1, 1:-1]
    chosen = jnp.stack(
        [
            center,
            padded[2:, 1:-1],
            padded[:-2, 1:-1],
            padded[1:-1, 2:],
            padded[1:-1, :-2],
            vup,
            vdown,
        ]
    ).astype(jnp.bfloat16).reshape(7, cells)
    h1 = jnp.tanh(jnp.dot(w_in, chosen, preferred_element_type=jnp.float32)).astype(jnp.bfloat16)
    h2 = jnp.tanh(jnp.dot(w_mid, h1, preferred_element_type=jnp.float32)).astype(jnp.bfloat16)
    corr = jnp.dot(w_out, h2, preferred_element_type=jnp.float32)[0] * weight
    dcl = (cotangent.reshape(cells) * weight).astype(jnp.bfloat16)
    h2f = h2.astype(jnp.float32)
    h1f = h1.astype(jnp.float32)
    dh2 = jnp.dot(w_out.T, dcl[None, :], preferred_element_type=jnp.float32)
    da2 = (dh2 * (1.0 - h2f * h2f)).astype(jnp.bfloat16)
    dh1 = jnp.dot(w_mid.T, da2, preferred_element_type=jnp.float32)
    da1 = (dh1 * (1.0 - h1f * h1f)).astype(jnp.bfloat16)
    dfeat = jnp.dot(w_in.T, da1, preferred_element_type=jnp.float32).reshape(7, sizex, sizey, sizez)
    dims = (((1,), (1,)), ((), ()))
    gmid = lax.dot_general(da2, h1, dims, preferred_element_type=jnp.float32)
    gout = lax.dot_general(dcl[None, :], h2, dims, preferred_element_type=jnp.float32)

    new_field = velocity + viscosity * padded_laplace(padded, vup, vdown) + corr.reshape(sizex, sizey, sizez)

    nx = lax.axis_size("gx")
    ny = lax.axis_size("gy")
    xodd = lax.axis_index("gx") % 2 == 1
    yodd = lax.axis_index("gy") % 2 == 1
    up_x, down_x = dfeat[1, -1], dfeat[2, 0]
    up_y, down_y = dfeat[3, :, -1], dfeat[4, :, 0]
    pair_face = {"gx": jnp.where(xodd, down_x, up_x), "gy": jnp.where(yodd, down_y, up_y)}
    other_x = lax.ppermute(
        jnp.where(xodd, up_x, down_x), "gx", [(i, (i + 1) % nx if i % 2 else (i - 1) % nx) for i in range(nx)]
    )
    other_y = lax.ppermute(
        jnp.where(yodd, up_y, down_y), "gy", [(i, (i + 1) % ny if i % 2 else (i - 1) % ny) for i in range(ny)]
    )

    gin_t = lax.dot_general(chosen, da1, dims, preferred_element_type=jnp.float32)
    grads = jnp.concatenate([gmid, gin_t, gout], axis=0)
    received = {}
    for pairs, tag in reduce_rounds(nx, ny):
        if tag is None:
            grads = grads + lax.ppermute(grads, ("gx", "gy"), pairs)
        else:
            rows = grads.shape[0]
            face = pair_face[tag]
            message = jnp.concatenate([grads, face.reshape(-1, grads.shape[1])], axis=0)
            got = lax.ppermute(message, ("gx", "gy"), pairs)
            received[tag] = got[rows:].reshape(face.shape)
            grads = grads + got[:rows]
    from_xlo = jnp.where(xodd, received["gx"], other_x)
    from_xhi = jnp.where(xodd, other_x, received["gx"])
    from_ylo = jnp.where(yodd, received["gy"], other_y)
    from_yhi = jnp.where(yodd, other_y, received["gy"])

    side1 = jnp.concatenate([from_xlo[None], dfeat[1, :-1]], axis=0)
    side2 = jnp.concatenate([dfeat[2, 1:], from_xhi[None]], axis=0)
    side3 = jnp.concatenate([from_ylo[:, None], dfeat[3, :, :-1]], axis=1)
    side4 = jnp.concatenate([dfeat[4, :, 1:], from_yhi[:, None]], axis=1)
    local = dfeat[0] + jnp.roll(dfeat[5], 1, 2) + jnp.roll(dfeat[6], -1, 2)
    grad_field = cotangent + viscosity * padded_laplace(cot_pad, cup, cdown) + local + (side1 + side2 + side3 + side4)

    scale = 1.0 / jnp.sqrt(jnp.float32(nx * ny * slots * 64))
    total = grads * scale
    width = gmid.shape[0]
    grad_mid = total[:width]
    grad_in = total[width : width + 7].T
    grad_out = total[width + 7 :]
    return (new_field, grad_field, grad_in, grad_mid, grad_out)


def solution(mesh):
    in_specs = (
        P("gx", "gy", None),
        P("gx", "gy", None),
        P("gx", "gy", None),
        P("gx", "gy"),
        P("gx", "gy", None),
        P(),
        P(),
        P(),
    )
    out_specs = (P("gx", "gy", None), P("gx", "gy", None), P(), P(), P())
    return jax.shard_map(body, mesh=mesh, in_specs=in_specs, out_specs=out_specs, check_vma=False)
```

```python
import jax
import jax.numpy as jnp
from jax import lax
from jax.sharding import PartitionSpec as P

viscosity = 0.1


def shift_from(face, axis, step):
    count = lax.axis_size(axis)
    return lax.ppermute(face, axis, [(i, (i + step) % count) for i in range(count)])


def reduce_rounds(nx, ny):
    if (nx, ny) == (64, 16):
        def decode(i):
            gx, gy = divmod(i, 16)
            return {"core": gx % 2, "x": (gx // 2) % 8, "y": (gy % 2) * 4 + gx // 16, "z": gy // 2}

        def encode(c):
            return ((c["y"] % 4) * 16 + c["x"] * 2 + c["core"]) * 16 + c["z"] * 2 + c["y"] // 4

        plan = [
            ("x", lambda v: v ^ 1, None),
            ("core", lambda v: v ^ 1, "gx"),
            ("y", lambda v: v ^ 4, "gy"),
            ("x", lambda v: v ^ 2, None),
            ("x", lambda v: 7 - v, None),
            ("y", lambda v: v ^ 1, None),
            ("y", lambda v: v ^ 2, None),
            ("z", lambda v: v ^ 1, None),
            ("z", lambda v: v ^ 2, None),
            ("z", lambda v: 7 - v, None),
        ]
        rounds = []
        for ring, step, tag in plan:
            pairs = []
            for i in range(nx * ny):
                c = decode(i)
                c[ring] = step(c[ring])
                pairs.append((i, encode(c)))
            rounds.append((pairs, tag))
        return rounds
    rounds = []
    for size, stride, tag in ((nx, ny, "gx"), (ny, 1, "gy")):
        for bit in range(size.bit_length() - 1):
            pairs = []
            for i in range(nx * ny):
                index = (i // stride) % size
                pairs.append((i, i + ((index ^ (1 << bit)) - index) * stride))
            rounds.append((pairs, tag if bit == 0 else None))
    return rounds


def from_blocks(blocks, sizex, sizey, sizez):
    lead = blocks.shape[:-2]
    count = len(lead)
    shaped = blocks.reshape(lead + (sizex // 4, sizey // 4, sizez // 4, 4, 4, 4))
    order = list(range(count)) + [count, count + 3, count + 1, count + 4, count + 2, count + 5]
    return shaped.transpose(order).reshape(lead + (sizex, sizey, sizez))


def padded_of(center, xlo, xhi, ylo, yhi):
    sizez = center.shape[-1]
    corner = jnp.zeros(center.shape[:-3] + (1, 1, sizez), center.dtype)
    mid = jnp.concatenate([ylo[..., :, None, :], center, yhi[..., :, None, :]], axis=-2)
    top = jnp.concatenate([corner, xlo[..., None, :, :], corner], axis=-2)
    bot = jnp.concatenate([corner, xhi[..., None, :, :], corner], axis=-2)
    return jnp.concatenate([top, mid, bot], axis=-3)


def padded_laplace(padded):
    center = padded[1:-1, 1:-1]
    total = padded[2:, 1:-1] + padded[:-2, 1:-1] + padded[1:-1, 2:] + padded[1:-1, :-2]
    total = total + jnp.roll(center, -1, 2) + jnp.roll(center, 1, 2)
    return total - 6.0 * center


def body(velocity, cotangent, block_ids, fluid_count, fluid_cells, w_in, w_mid, w_out):
    sizex, sizey, sizez = velocity.shape
    slots = block_ids.shape[2]
    nblocks = sizex * sizey * sizez // 64
    cells = sizex * sizey * sizez

    both = jnp.stack([velocity, cotangent])
    xlo = shift_from(both[:, -1], "gx", 1)
    xhi = shift_from(both[:, 0], "gx", -1)
    ylo = shift_from(both[:, :, -1], "gy", 1)
    yhi = shift_from(both[:, :, 0], "gy", -1)
    padded = padded_of(velocity, xlo[0], xhi[0], ylo[0], yhi[0])
    cot_pad = padded_of(cotangent, xlo[1], xhi[1], ylo[1], yhi[1])

    ids = block_ids.reshape(slots)
    live = (jnp.arange(slots) < fluid_count[0, 0]).astype(jnp.bfloat16)
    slot_w = fluid_cells.reshape(slots, 64).astype(jnp.bfloat16) * live[:, None]
    onehot = (ids[:, None] == jnp.arange(nblocks)[None, :]).astype(jnp.bfloat16)
    block_w = lax.dot_general(onehot, slot_w, (((0,), (0,)), ((), ())), preferred_element_type=jnp.float32)
    weight = from_blocks(block_w, sizex, sizey, sizez).reshape(cells)

    center = padded[1:-1, 1:-1]
    chosen = jnp.stack(
        [
            center,
            padded[2:, 1:-1],
            padded[:-2, 1:-1],
            padded[1:-1, 2:],
            padded[1:-1, :-2],
            jnp.roll(center, -1, 2),
            jnp.roll(center, 1, 2),
        ]
    ).astype(jnp.bfloat16).reshape(7, cells)
    h1 = jnp.tanh(jnp.dot(w_in, chosen, preferred_element_type=jnp.float32)).astype(jnp.bfloat16)
    h2 = jnp.tanh(jnp.dot(w_mid, h1, preferred_element_type=jnp.float32)).astype(jnp.bfloat16)
    corr = jnp.dot(w_out, h2, preferred_element_type=jnp.float32)[0] * weight
    dcl = (cotangent.reshape(cells) * weight).astype(jnp.bfloat16)
    h2f = h2.astype(jnp.float32)
    h1f = h1.astype(jnp.float32)
    dh2 = jnp.dot(w_out.T, dcl[None, :], preferred_element_type=jnp.float32)
    da2 = (dh2 * (1.0 - h2f * h2f)).astype(jnp.bfloat16)
    dh1 = jnp.dot(w_mid.T, da2, preferred_element_type=jnp.float32)
    da1 = (dh1 * (1.0 - h1f * h1f)).astype(jnp.bfloat16)
    dfeat = jnp.dot(w_in.T, da1, preferred_element_type=jnp.float32).reshape(7, sizex, sizey, sizez)
    dims = (((1,), (1,)), ((), ()))
    gmid = lax.dot_general(da2, h1, dims, preferred_element_type=jnp.float32)
    gout = lax.dot_general(dcl[None, :], h2, dims, preferred_element_type=jnp.float32)

    new_field = velocity + viscosity * padded_laplace(padded) + corr.reshape(sizex, sizey, sizez)

    nx = lax.axis_size("gx")
    ny = lax.axis_size("gy")
    xodd = lax.axis_index("gx") % 2 == 1
    yodd = lax.axis_index("gy") % 2 == 1
    up_x, down_x = dfeat[1, -1], dfeat[2, 0]
    up_y, down_y = dfeat[3, :, -1], dfeat[4, :, 0]
    pair_face = {"gx": jnp.where(xodd, down_x, up_x), "gy": jnp.where(yodd, down_y, up_y)}
    other_x = lax.ppermute(
        jnp.where(xodd, up_x, down_x), "gx", [(i, (i + 1) % nx if i % 2 else (i - 1) % nx) for i in range(nx)]
    )
    other_y = lax.ppermute(
        jnp.where(yodd, up_y, down_y), "gy", [(i, (i + 1) % ny if i % 2 else (i - 1) % ny) for i in range(ny)]
    )

    gin_t = lax.dot_general(chosen, da1, dims, preferred_element_type=jnp.float32)
    width = gmid.shape[0]
    lanes = 128
    grads = jnp.concatenate(
        [gmid.reshape(-1, lanes), jnp.concatenate([gin_t, gout], axis=0).reshape(-1, lanes)], axis=0
    )
    received = {}
    for pairs, tag in reduce_rounds(nx, ny):
        if tag is None:
            grads = grads + lax.ppermute(grads, ("gx", "gy"), pairs)
        else:
            rows = grads.shape[0]
            face = pair_face[tag]
            message = jnp.concatenate([grads, face.reshape(-1, grads.shape[1])], axis=0)
            got = lax.ppermute(message, ("gx", "gy"), pairs)
            received[tag] = got[rows:].reshape(face.shape)
            grads = grads + got[:rows]
    from_xlo = jnp.where(xodd, received["gx"], other_x)
    from_xhi = jnp.where(xodd, other_x, received["gx"])
    from_ylo = jnp.where(yodd, received["gy"], other_y)
    from_yhi = jnp.where(yodd, other_y, received["gy"])

    side1 = jnp.concatenate([from_xlo[None], dfeat[1, :-1]], axis=0)
    side2 = jnp.concatenate([dfeat[2, 1:], from_xhi[None]], axis=0)
    side3 = jnp.concatenate([from_ylo[:, None], dfeat[3, :, :-1]], axis=1)
    side4 = jnp.concatenate([dfeat[4, :, 1:], from_yhi[:, None]], axis=1)
    local = dfeat[0] + jnp.roll(dfeat[5], 1, 2) + jnp.roll(dfeat[6], -1, 2)
    grad_field = cotangent + viscosity * padded_laplace(cot_pad) + local + (side1 + side2 + side3 + side4)

    scale = 1.0 / jnp.sqrt(jnp.float32(nx * ny * slots * 64))
    total = grads * scale
    mid_rows = width * width // lanes
    grad_mid = total[:mid_rows].reshape(width, width)
    rest = total[mid_rows:].reshape(-1, width)
    grad_in = rest[:7].T
    grad_out = rest[7:8]
    return (new_field, grad_field, grad_in, grad_mid, grad_out)


def solution(mesh):
    in_specs = (
        P("gx", "gy", None),
        P("gx", "gy", None),
        P("gx", "gy", None),
        P("gx", "gy"),
        P("gx", "gy", None),
        P(),
        P(),
        P(),
    )
    out_specs = (P("gx", "gy", None), P("gx", "gy", None), P(), P(), P())
    return jax.shard_map(body, mesh=mesh, in_specs=in_specs, out_specs=out_specs, check_vma=False)
```

```python
import jax
import jax.numpy as jnp
from jax import lax
from jax.sharding import PartitionSpec as P

viscosity = 0.1


def shift_from(face, axis, step):
    count = lax.axis_size(axis)
    return lax.ppermute(face, axis, [(i, (i + step) % count) for i in range(count)])


def reduce_rounds(nx, ny):
    if (nx, ny) == (64, 16):
        def decode(i):
            gx, gy = divmod(i, 16)
            return {"core": gx % 2, "x": (gx // 2) % 8, "y": (gy % 2) * 4 + gx // 16, "z": gy // 2}

        def encode(c):
            return ((c["y"] % 4) * 16 + c["x"] * 2 + c["core"]) * 16 + c["z"] * 2 + c["y"] // 4

        plan = [
            ("x", lambda v: v ^ 1, None),
            ("core", lambda v: v ^ 1, "gx"),
            ("y", lambda v: v ^ 4, "gy"),
            ("x", lambda v: v ^ 2, None),
            ("x", lambda v: v ^ 6, None),
            ("y", lambda v: v ^ 1, None),
            ("y", lambda v: v ^ 2, None),
            ("z", lambda v: v ^ 1, None),
            ("z", lambda v: v ^ 2, None),
            ("z", lambda v: v ^ 6, None),
        ]
        rounds = []
        for ring, step, tag in plan:
            pairs = []
            for i in range(nx * ny):
                c = decode(i)
                c[ring] = step(c[ring])
                pairs.append((i, encode(c)))
            rounds.append((pairs, tag))
        return rounds
    rounds = []
    for size, stride, tag in ((nx, ny, "gx"), (ny, 1, "gy")):
        for bit in range(size.bit_length() - 1):
            pairs = []
            for i in range(nx * ny):
                index = (i // stride) % size
                pairs.append((i, i + ((index ^ (1 << bit)) - index) * stride))
            rounds.append((pairs, tag if bit == 0 else None))
    return rounds


def from_blocks(blocks, sizex, sizey, sizez):
    lead = blocks.shape[:-2]
    count = len(lead)
    shaped = blocks.reshape(lead + (sizex // 4, sizey // 4, sizez // 4, 4, 4, 4))
    order = list(range(count)) + [count, count + 3, count + 1, count + 4, count + 2, count + 5]
    return shaped.transpose(order).reshape(lead + (sizex, sizey, sizez))


def padded_of(center, xlo, xhi, ylo, yhi):
    sizez = center.shape[-1]
    corner = jnp.zeros(center.shape[:-3] + (1, 1, sizez), center.dtype)
    mid = jnp.concatenate([ylo[..., :, None, :], center, yhi[..., :, None, :]], axis=-2)
    top = jnp.concatenate([corner, xlo[..., None, :, :], corner], axis=-2)
    bot = jnp.concatenate([corner, xhi[..., None, :, :], corner], axis=-2)
    return jnp.concatenate([top, mid, bot], axis=-3)


def padded_laplace(padded):
    center = padded[1:-1, 1:-1]
    total = padded[2:, 1:-1] + padded[:-2, 1:-1] + padded[1:-1, 2:] + padded[1:-1, :-2]
    total = total + jnp.roll(center, -1, 2) + jnp.roll(center, 1, 2)
    return total - 6.0 * center


def body(velocity, cotangent, block_ids, fluid_count, fluid_cells, w_in, w_mid, w_out):
    sizex, sizey, sizez = velocity.shape
    slots = block_ids.shape[2]
    nblocks = sizex * sizey * sizez // 64
    cells = sizex * sizey * sizez

    both = jnp.stack([velocity, cotangent])
    xlo = shift_from(both[:, -1], "gx", 1)
    xhi = shift_from(both[:, 0], "gx", -1)
    ylo = shift_from(both[:, :, -1], "gy", 1)
    yhi = shift_from(both[:, :, 0], "gy", -1)
    padded = padded_of(velocity, xlo[0], xhi[0], ylo[0], yhi[0])
    cot_pad = padded_of(cotangent, xlo[1], xhi[1], ylo[1], yhi[1])

    ids = block_ids.reshape(slots)
    live = (jnp.arange(slots) < fluid_count[0, 0]).astype(jnp.bfloat16)
    slot_w = fluid_cells.reshape(slots, 64).astype(jnp.bfloat16) * live[:, None]
    onehot = (ids[:, None] == jnp.arange(nblocks)[None, :]).astype(jnp.bfloat16)
    block_w = lax.dot_general(onehot, slot_w, (((0,), (0,)), ((), ())), preferred_element_type=jnp.float32)
    weight = from_blocks(block_w, sizex, sizey, sizez).reshape(cells)

    center = padded[1:-1, 1:-1]
    chosen = jnp.stack(
        [
            center,
            padded[2:, 1:-1],
            padded[:-2, 1:-1],
            padded[1:-1, 2:],
            padded[1:-1, :-2],
            jnp.roll(center, -1, 2),
            jnp.roll(center, 1, 2),
        ]
    ).astype(jnp.bfloat16).reshape(7, cells)
    h1 = jnp.tanh(jnp.dot(w_in, chosen, preferred_element_type=jnp.float32)).astype(jnp.bfloat16)
    h2 = jnp.tanh(jnp.dot(w_mid, h1, preferred_element_type=jnp.float32)).astype(jnp.bfloat16)
    corr = jnp.dot(w_out, h2, preferred_element_type=jnp.float32)[0] * weight
    dcl = (cotangent.reshape(cells) * weight).astype(jnp.bfloat16)
    h2f = h2.astype(jnp.float32)
    h1f = h1.astype(jnp.float32)
    dh2 = jnp.dot(w_out.T, dcl[None, :], preferred_element_type=jnp.float32)
    da2 = (dh2 * (1.0 - h2f * h2f)).astype(jnp.bfloat16)
    dh1 = jnp.dot(w_mid.T, da2, preferred_element_type=jnp.float32)
    da1 = (dh1 * (1.0 - h1f * h1f)).astype(jnp.bfloat16)
    dfeat = jnp.dot(w_in.T, da1, preferred_element_type=jnp.float32).reshape(7, sizex, sizey, sizez)
    dims = (((1,), (1,)), ((), ()))
    gmid = lax.dot_general(da2, h1, dims, preferred_element_type=jnp.float32)
    gout = lax.dot_general(dcl[None, :], h2, dims, preferred_element_type=jnp.float32)

    new_field = velocity + viscosity * padded_laplace(padded) + corr.reshape(sizex, sizey, sizez)

    nx = lax.axis_size("gx")
    ny = lax.axis_size("gy")
    xodd = lax.axis_index("gx") % 2 == 1
    yodd = lax.axis_index("gy") % 2 == 1
    up_x, down_x = dfeat[1, -1], dfeat[2, 0]
    up_y, down_y = dfeat[3, :, -1], dfeat[4, :, 0]
    pair_face = {"gx": jnp.where(xodd, down_x, up_x), "gy": jnp.where(yodd, down_y, up_y)}
    other_x = lax.ppermute(
        jnp.where(xodd, up_x, down_x), "gx", [(i, (i + 1) % nx if i % 2 else (i - 1) % nx) for i in range(nx)]
    )
    other_y = lax.ppermute(
        jnp.where(yodd, up_y, down_y), "gy", [(i, (i + 1) % ny if i % 2 else (i - 1) % ny) for i in range(ny)]
    )

    gin_t = lax.dot_general(chosen, da1, dims, preferred_element_type=jnp.float32)
    width = gmid.shape[0]
    lanes = 128
    grads = jnp.concatenate(
        [gmid.reshape(-1, lanes), jnp.concatenate([gin_t, gout], axis=0).reshape(-1, lanes)], axis=0
    )
    received = {}
    for pairs, tag in reduce_rounds(nx, ny):
        if tag is None:
            grads = grads + lax.ppermute(grads, ("gx", "gy"), pairs)
        else:
            rows = grads.shape[0]
            face = pair_face[tag]
            message = jnp.concatenate([grads, face.reshape(-1, grads.shape[1])], axis=0)
            got = lax.ppermute(message, ("gx", "gy"), pairs)
            received[tag] = got[rows:].reshape(face.shape)
            grads = grads + got[:rows]
    from_xlo = jnp.where(xodd, received["gx"], other_x)
    from_xhi = jnp.where(xodd, other_x, received["gx"])
    from_ylo = jnp.where(yodd, received["gy"], other_y)
    from_yhi = jnp.where(yodd, other_y, received["gy"])

    side1 = jnp.concatenate([from_xlo[None], dfeat[1, :-1]], axis=0)
    side2 = jnp.concatenate([dfeat[2, 1:], from_xhi[None]], axis=0)
    side3 = jnp.concatenate([from_ylo[:, None], dfeat[3, :, :-1]], axis=1)
    side4 = jnp.concatenate([dfeat[4, :, 1:], from_yhi[:, None]], axis=1)
    local = dfeat[0] + jnp.roll(dfeat[5], 1, 2) + jnp.roll(dfeat[6], -1, 2)
    grad_field = cotangent + viscosity * padded_laplace(cot_pad) + local + (side1 + side2 + side3 + side4)

    scale = 1.0 / jnp.sqrt(jnp.float32(nx * ny * slots * 64))
    total = grads * scale
    mid_rows = width * width // lanes
    grad_mid = total[:mid_rows].reshape(width, width)
    rest = total[mid_rows:].reshape(-1, width)
    grad_in = rest[:7].T
    grad_out = rest[7:8]
    return (new_field, grad_field, grad_in, grad_mid, grad_out)


def solution(mesh):
    in_specs = (
        P("gx", "gy", None),
        P("gx", "gy", None),
        P("gx", "gy", None),
        P("gx", "gy"),
        P("gx", "gy", None),
        P(),
        P(),
        P(),
    )
    out_specs = (P("gx", "gy", None), P("gx", "gy", None), P(), P(), P())
    return jax.shard_map(body, mesh=mesh, in_specs=in_specs, out_specs=out_specs, check_vma=False)
```

```python
import jax
import jax.numpy as jnp
from jax import lax
from jax.sharding import PartitionSpec as P

viscosity = 0.1


def shift_from(face, axis, step):
    count = lax.axis_size(axis)
    return lax.ppermute(face, axis, [(i, (i + step) % count) for i in range(count)])


def reduce_rounds(nx, ny):
    if (nx, ny) == (64, 16):
        def decode(i):
            gx, gy = divmod(i, 16)
            return {"core": gx % 2, "x": (gx // 2) % 8, "y": (gy % 2) * 4 + gx // 16, "z": gy // 2}

        def encode(c):
            return ((c["y"] % 4) * 16 + c["x"] * 2 + c["core"]) * 16 + c["z"] * 2 + c["y"] // 4

        plan = [
            ("x", lambda v: v ^ 1, None),
            ("core", lambda v: v ^ 1, "gx"),
            ("y", lambda v: v ^ 4, "gy"),
            ("x", lambda v: v ^ 2, None),
            ("x", lambda v: 7 - v, None),
            ("y", lambda v: v ^ 1, None),
            ("y", lambda v: v ^ 2, None),
            ("z", lambda v: v ^ 1, None),
            ("z", lambda v: v ^ 2, None),
            ("z", lambda v: 7 - v, None),
        ]
        rounds = []
        for ring, step, tag in plan:
            pairs = []
            for i in range(nx * ny):
                c = decode(i)
                c[ring] = step(c[ring])
                pairs.append((i, encode(c)))
            rounds.append((pairs, tag))
        return rounds
    rounds = []
    for size, stride, tag in ((nx, ny, "gx"), (ny, 1, "gy")):
        for bit in range(size.bit_length() - 1):
            pairs = []
            for i in range(nx * ny):
                index = (i // stride) % size
                pairs.append((i, i + ((index ^ (1 << bit)) - index) * stride))
            rounds.append((pairs, tag if bit == 0 else None))
    return rounds


def from_blocks(blocks, sizex, sizey, sizez):
    lead = blocks.shape[:-2]
    count = len(lead)
    shaped = blocks.reshape(lead + (sizex // 4, sizey // 4, sizez // 4, 4, 4, 4))
    order = list(range(count)) + [count, count + 3, count + 1, count + 4, count + 2, count + 5]
    return shaped.transpose(order).reshape(lead + (sizex, sizey, sizez))


def padded_of(center, xlo, xhi, ylo, yhi):
    sizez = center.shape[-1]
    corner = jnp.zeros(center.shape[:-3] + (1, 1, sizez), center.dtype)
    mid = jnp.concatenate([ylo[..., :, None, :], center, yhi[..., :, None, :]], axis=-2)
    top = jnp.concatenate([corner, xlo[..., None, :, :], corner], axis=-2)
    bot = jnp.concatenate([corner, xhi[..., None, :, :], corner], axis=-2)
    return jnp.concatenate([top, mid, bot], axis=-3)


def padded_laplace(padded, zup, zdown):
    center = padded[1:-1, 1:-1]
    total = padded[2:, 1:-1] + padded[:-2, 1:-1] + padded[1:-1, 2:] + padded[1:-1, :-2]
    total = total + zup + zdown
    return total - 6.0 * center


def z_neighbours(field):
    sizez = field.shape[-1]
    rows = lax.broadcasted_iota(jnp.int32, (sizez, 2 * sizez), 0)
    cols = lax.broadcasted_iota(jnp.int32, (sizez, 2 * sizez), 1)
    source = jnp.where(cols < sizez, (cols + 1) % sizez, (cols - sizez - 1) % sizez)
    shift = (rows == source).astype(field.dtype)
    both = jnp.dot(field.reshape(-1, sizez), shift, precision=lax.Precision.HIGHEST, preferred_element_type=jnp.float32)
    return both[:, :sizez].reshape(field.shape), both[:, sizez:].reshape(field.shape)


def body(velocity, cotangent, block_ids, fluid_count, fluid_cells, w_in, w_mid, w_out):
    sizex, sizey, sizez = velocity.shape
    slots = block_ids.shape[2]
    nblocks = sizex * sizey * sizez // 64
    cells = sizex * sizey * sizez

    both = jnp.stack([velocity, cotangent])
    xlo = shift_from(both[:, -1], "gx", 1)
    xhi = shift_from(both[:, 0], "gx", -1)
    ylo = shift_from(both[:, :, -1], "gy", 1)
    yhi = shift_from(both[:, :, 0], "gy", -1)
    padded = padded_of(velocity, xlo[0], xhi[0], ylo[0], yhi[0])
    cot_pad = padded_of(cotangent, xlo[1], xhi[1], ylo[1], yhi[1])

    ids = block_ids.reshape(slots)
    live = (jnp.arange(slots) < fluid_count[0, 0]).astype(jnp.bfloat16)
    slot_w = fluid_cells.reshape(slots, 64).astype(jnp.bfloat16) * live[:, None]
    onehot = (ids[:, None] == jnp.arange(nblocks)[None, :]).astype(jnp.bfloat16)
    block_w = lax.dot_general(onehot, slot_w, (((0,), (0,)), ((), ())), preferred_element_type=jnp.float32)
    weight = from_blocks(block_w, sizex, sizey, sizez).reshape(cells)

    center = padded[1:-1, 1:-1]
    vup, vdown = z_neighbours(velocity)
    cup, cdown = z_neighbours(cotangent)
    chosen = jnp.stack(
        [
            center,
            padded[2:, 1:-1],
            padded[:-2, 1:-1],
            padded[1:-1, 2:],
            padded[1:-1, :-2],
            vup,
            vdown,
        ]
    ).astype(jnp.bfloat16).reshape(7, cells)
    h1 = jnp.tanh(jnp.dot(w_in, chosen, preferred_element_type=jnp.float32)).astype(jnp.bfloat16)
    h2 = jnp.tanh(jnp.dot(w_mid, h1, preferred_element_type=jnp.float32)).astype(jnp.bfloat16)
    corr = jnp.dot(w_out, h2, preferred_element_type=jnp.float32)[0] * weight
    dcl = (cotangent.reshape(cells) * weight).astype(jnp.bfloat16)
    h2f = h2.astype(jnp.float32)
    h1f = h1.astype(jnp.float32)
    dh2 = jnp.dot(w_out.T, dcl[None, :], preferred_element_type=jnp.float32)
    da2 = (dh2 * (1.0 - h2f * h2f)).astype(jnp.bfloat16)
    dh1 = jnp.dot(w_mid.T, da2, preferred_element_type=jnp.float32)
    da1 = (dh1 * (1.0 - h1f * h1f)).astype(jnp.bfloat16)
    dfeat = jnp.dot(w_in.T, da1, preferred_element_type=jnp.float32).reshape(7, sizex, sizey, sizez)
    dims = (((1,), (1,)), ((), ()))
    gmid = lax.dot_general(da2, h1, dims, preferred_element_type=jnp.float32)
    gout = lax.dot_general(dcl[None, :], h2, dims, preferred_element_type=jnp.float32)

    new_field = velocity + viscosity * padded_laplace(padded, vup, vdown) + corr.reshape(sizex, sizey, sizez)

    nx = lax.axis_size("gx")
    ny = lax.axis_size("gy")
    xodd = lax.axis_index("gx") % 2 == 1
    yodd = lax.axis_index("gy") % 2 == 1
    up_x, down_x = dfeat[1, -1], dfeat[2, 0]
    up_y, down_y = dfeat[3, :, -1], dfeat[4, :, 0]
    pair_face = {"gx": jnp.where(xodd, down_x, up_x), "gy": jnp.where(yodd, down_y, up_y)}
    other_x = lax.ppermute(
        jnp.where(xodd, up_x, down_x), "gx", [(i, (i + 1) % nx if i % 2 else (i - 1) % nx) for i in range(nx)]
    )
    other_y = lax.ppermute(
        jnp.where(yodd, up_y, down_y), "gy", [(i, (i + 1) % ny if i % 2 else (i - 1) % ny) for i in range(ny)]
    )

    gin_t = lax.dot_general(chosen, da1, dims, preferred_element_type=jnp.float32)
    width = gmid.shape[0]
    lanes = 128
    grads = jnp.concatenate(
        [gmid.reshape(-1, lanes), jnp.concatenate([gin_t, gout], axis=0).reshape(-1, lanes)], axis=0
    )
    received = {}
    for pairs, tag in reduce_rounds(nx, ny):
        if tag is None:
            grads = grads + lax.ppermute(grads, ("gx", "gy"), pairs)
        else:
            rows = grads.shape[0]
            face = pair_face[tag]
            message = jnp.concatenate([grads, face.reshape(-1, grads.shape[1])], axis=0)
            got = lax.ppermute(message, ("gx", "gy"), pairs)
            received[tag] = got[rows:].reshape(face.shape)
            grads = grads + got[:rows]
    from_xlo = jnp.where(xodd, received["gx"], other_x)
    from_xhi = jnp.where(xodd, other_x, received["gx"])
    from_ylo = jnp.where(yodd, received["gy"], other_y)
    from_yhi = jnp.where(yodd, other_y, received["gy"])

    side1 = jnp.concatenate([from_xlo[None], dfeat[1, :-1]], axis=0)
    side2 = jnp.concatenate([dfeat[2, 1:], from_xhi[None]], axis=0)
    side3 = jnp.concatenate([from_ylo[:, None], dfeat[3, :, :-1]], axis=1)
    side4 = jnp.concatenate([dfeat[4, :, 1:], from_yhi[:, None]], axis=1)
    local = dfeat[0] + jnp.roll(dfeat[5], 1, 2) + jnp.roll(dfeat[6], -1, 2)
    grad_field = cotangent + viscosity * padded_laplace(cot_pad, cup, cdown) + local + (side1 + side2 + side3 + side4)

    scale = 1.0 / jnp.sqrt(jnp.float32(nx * ny * slots * 64))
    total = grads * scale
    mid_rows = width * width // lanes
    grad_mid = total[:mid_rows].reshape(width, width)
    rest = total[mid_rows:].reshape(-1, width)
    grad_in = rest[:7].T
    grad_out = rest[7:8]
    return (new_field, grad_field, grad_in, grad_mid, grad_out)


def solution(mesh):
    in_specs = (
        P("gx", "gy", None),
        P("gx", "gy", None),
        P("gx", "gy", None),
        P("gx", "gy"),
        P("gx", "gy", None),
        P(),
        P(),
        P(),
    )
    out_specs = (P("gx", "gy", None), P("gx", "gy", None), P(), P(), P())
    return jax.shard_map(body, mesh=mesh, in_specs=in_specs, out_specs=out_specs, check_vma=False)
```

```python
import jax
import jax.numpy as jnp
from jax import lax
from jax.sharding import PartitionSpec as P

viscosity = 0.1


def shift_from(face, axis, step):
    count = lax.axis_size(axis)
    return lax.ppermute(face, axis, [(i, (i + step) % count) for i in range(count)])


def reduce_rounds(nx, ny):
    if (nx, ny) == (64, 16):
        def decode(i):
            gx, gy = divmod(i, 16)
            return {"core": gx % 2, "x": (gx // 2) % 8, "y": (gy % 2) * 4 + gx // 16, "z": gy // 2}

        def encode(c):
            return ((c["y"] % 4) * 16 + c["x"] * 2 + c["core"]) * 16 + c["z"] * 2 + c["y"] // 4

        plan = [
            ("x", lambda v: v ^ 1, None),
            ("core", lambda v: v ^ 1, "gx"),
            ("y", lambda v: v ^ 4, "gy"),
            ("x", lambda v: v ^ 2, None),
            ("x", lambda v: 7 - v, None),
            ("y", lambda v: v ^ 1, None),
            ("y", lambda v: v ^ 2, None),
            ("z", lambda v: v ^ 1, None),
            ("z", lambda v: v ^ 2, None),
            ("z", lambda v: 7 - v, None),
        ]
        rounds = []
        for ring, step, tag in plan:
            pairs = []
            for i in range(nx * ny):
                c = decode(i)
                c[ring] = step(c[ring])
                pairs.append((i, encode(c)))
            rounds.append((pairs, tag))
        return rounds
    rounds = []
    for size, stride, tag in ((nx, ny, "gx"), (ny, 1, "gy")):
        for bit in range(size.bit_length() - 1):
            pairs = []
            for i in range(nx * ny):
                index = (i // stride) % size
                pairs.append((i, i + ((index ^ (1 << bit)) - index) * stride))
            rounds.append((pairs, tag if bit == 0 else None))
    return rounds


def from_blocks(blocks, sizex, sizey, sizez):
    lead = blocks.shape[:-2]
    count = len(lead)
    shaped = blocks.reshape(lead + (sizex // 4, sizey // 4, sizez // 4, 4, 4, 4))
    order = list(range(count)) + [count, count + 3, count + 1, count + 4, count + 2, count + 5]
    return shaped.transpose(order).reshape(lead + (sizex, sizey, sizez))


def padded_of(center, xlo, xhi, ylo, yhi):
    sizez = center.shape[-1]
    corner = jnp.zeros(center.shape[:-3] + (1, 1, sizez), center.dtype)
    mid = jnp.concatenate([ylo[..., :, None, :], center, yhi[..., :, None, :]], axis=-2)
    top = jnp.concatenate([corner, xlo[..., None, :, :], corner], axis=-2)
    bot = jnp.concatenate([corner, xhi[..., None, :, :], corner], axis=-2)
    return jnp.concatenate([top, mid, bot], axis=-3)


def padded_laplace(padded, zup, zdown):
    center = padded[1:-1, 1:-1]
    total = padded[2:, 1:-1] + padded[:-2, 1:-1] + padded[1:-1, 2:] + padded[1:-1, :-2]
    total = total + zup + zdown
    return total - 6.0 * center


def z_neighbours(field):
    sizez = field.shape[-1]
    rows = lax.broadcasted_iota(jnp.int32, (sizez, 2 * sizez), 0)
    cols = lax.broadcasted_iota(jnp.int32, (sizez, 2 * sizez), 1)
    source = jnp.where(cols < sizez, (cols + 1) % sizez, (cols - sizez - 1) % sizez)
    shift = (rows == source).astype(field.dtype)
    both = jnp.dot(field.reshape(-1, sizez), shift, precision=lax.Precision.HIGHEST, preferred_element_type=jnp.float32)
    return both[:, :sizez].reshape(field.shape), both[:, sizez:].reshape(field.shape)


def body(velocity, cotangent, block_ids, fluid_count, fluid_cells, w_in, w_mid, w_out):
    sizex, sizey, sizez = velocity.shape
    slots = block_ids.shape[2]
    nblocks = sizex * sizey * sizez // 64
    cells = sizex * sizey * sizez

    both = jnp.stack([velocity, cotangent])
    xlo = shift_from(both[:, -1], "gx", 1)
    xhi = shift_from(both[:, 0], "gx", -1)
    ylo = shift_from(both[:, :, -1], "gy", 1)
    yhi = shift_from(both[:, :, 0], "gy", -1)
    padded = padded_of(velocity, xlo[0], xhi[0], ylo[0], yhi[0])
    cot_pad = padded_of(cotangent, xlo[1], xhi[1], ylo[1], yhi[1])

    ids = block_ids.reshape(slots)
    live = (jnp.arange(slots) < fluid_count[0, 0]).astype(jnp.bfloat16)
    slot_w = fluid_cells.reshape(slots, 64).astype(jnp.bfloat16) * live[:, None]
    onehot = (ids[:, None] == jnp.arange(nblocks)[None, :]).astype(jnp.bfloat16)
    block_w = lax.dot_general(onehot, slot_w, (((0,), (0,)), ((), ())), preferred_element_type=jnp.float32)
    grid = (sizex * sizey, sizez)
    weight = from_blocks(block_w, sizex, sizey, sizez).reshape(grid)

    center = padded[1:-1, 1:-1]
    vup, vdown = z_neighbours(velocity)
    cup, cdown = z_neighbours(cotangent)
    chosen = jnp.stack(
        [
            center,
            padded[2:, 1:-1],
            padded[:-2, 1:-1],
            padded[1:-1, 2:],
            padded[1:-1, :-2],
            vup,
            vdown,
        ]
    ).astype(jnp.bfloat16).reshape((7,) + grid)
    def mix(w, a):
        return jnp.einsum("oc,crz->orz", w, a, preferred_element_type=jnp.float32)

    h1 = jnp.tanh(mix(w_in, chosen)).astype(jnp.bfloat16)
    h2 = jnp.tanh(mix(w_mid, h1)).astype(jnp.bfloat16)
    corr = mix(w_out, h2)[0] * weight
    dcl = (cotangent.reshape(grid) * weight).astype(jnp.bfloat16)
    h2f = h2.astype(jnp.float32)
    h1f = h1.astype(jnp.float32)
    dh2 = mix(w_out.T, dcl[None])
    da2 = (dh2 * (1.0 - h2f * h2f)).astype(jnp.bfloat16)
    dh1 = mix(w_mid.T, da2)
    da1 = (dh1 * (1.0 - h1f * h1f)).astype(jnp.bfloat16)
    dfeat = mix(w_in.T, da1).reshape(7, sizex, sizey, sizez)
    dims = (((1, 2), (1, 2)), ((), ()))
    gmid = lax.dot_general(da2, h1, dims, preferred_element_type=jnp.float32)
    gout = lax.dot_general(dcl[None], h2, dims, preferred_element_type=jnp.float32)

    new_field = velocity + viscosity * padded_laplace(padded, vup, vdown) + corr.reshape(sizex, sizey, sizez)

    nx = lax.axis_size("gx")
    ny = lax.axis_size("gy")
    xodd = lax.axis_index("gx") % 2 == 1
    yodd = lax.axis_index("gy") % 2 == 1
    up_x, down_x = dfeat[1, -1], dfeat[2, 0]
    up_y, down_y = dfeat[3, :, -1], dfeat[4, :, 0]
    pair_face = {"gx": jnp.where(xodd, down_x, up_x), "gy": jnp.where(yodd, down_y, up_y)}
    other_x = lax.ppermute(
        jnp.where(xodd, up_x, down_x), "gx", [(i, (i + 1) % nx if i % 2 else (i - 1) % nx) for i in range(nx)]
    )
    other_y = lax.ppermute(
        jnp.where(yodd, up_y, down_y), "gy", [(i, (i + 1) % ny if i % 2 else (i - 1) % ny) for i in range(ny)]
    )

    gin_t = lax.dot_general(chosen, da1, dims, preferred_element_type=jnp.float32)
    width = gmid.shape[0]
    lanes = 128
    grads = jnp.concatenate(
        [gmid.reshape(-1, lanes), jnp.concatenate([gin_t, gout], axis=0).reshape(-1, lanes)], axis=0
    )
    received = {}
    for pairs, tag in reduce_rounds(nx, ny):
        if tag is None:
            grads = grads + lax.ppermute(grads, ("gx", "gy"), pairs)
        else:
            rows = grads.shape[0]
            face = pair_face[tag]
            message = jnp.concatenate([grads, face.reshape(-1, grads.shape[1])], axis=0)
            got = lax.ppermute(message, ("gx", "gy"), pairs)
            received[tag] = got[rows:].reshape(face.shape)
            grads = grads + got[:rows]
    from_xlo = jnp.where(xodd, received["gx"], other_x)
    from_xhi = jnp.where(xodd, other_x, received["gx"])
    from_ylo = jnp.where(yodd, received["gy"], other_y)
    from_yhi = jnp.where(yodd, other_y, received["gy"])

    side1 = jnp.concatenate([from_xlo[None], dfeat[1, :-1]], axis=0)
    side2 = jnp.concatenate([dfeat[2, 1:], from_xhi[None]], axis=0)
    side3 = jnp.concatenate([from_ylo[:, None], dfeat[3, :, :-1]], axis=1)
    side4 = jnp.concatenate([dfeat[4, :, 1:], from_yhi[:, None]], axis=1)
    local = dfeat[0] + jnp.roll(dfeat[5], 1, 2) + jnp.roll(dfeat[6], -1, 2)
    grad_field = cotangent + viscosity * padded_laplace(cot_pad, cup, cdown) + local + (side1 + side2 + side3 + side4)

    scale = 1.0 / jnp.sqrt(jnp.float32(nx * ny * slots * 64))
    total = grads * scale
    mid_rows = width * width // lanes
    grad_mid = total[:mid_rows].reshape(width, width)
    rest = total[mid_rows:].reshape(-1, width)
    grad_in = rest[:7].T
    grad_out = rest[7:8]
    return (new_field, grad_field, grad_in, grad_mid, grad_out)


def solution(mesh):
    in_specs = (
        P("gx", "gy", None),
        P("gx", "gy", None),
        P("gx", "gy", None),
        P("gx", "gy"),
        P("gx", "gy", None),
        P(),
        P(),
        P(),
    )
    out_specs = (P("gx", "gy", None), P("gx", "gy", None), P(), P(), P())
    return jax.shard_map(body, mesh=mesh, in_specs=in_specs, out_specs=out_specs, check_vma=False)
```

```python
import jax
import jax.numpy as jnp
from jax import lax
from jax.sharding import PartitionSpec as P

viscosity = 0.1


def shift_from(face, axis, step):
    count = lax.axis_size(axis)
    return lax.ppermute(face, axis, [(i, (i + step) % count) for i in range(count)])


def reduce_rounds(nx, ny):
    if (nx, ny) == (64, 16):
        def decode(i):
            gx, gy = divmod(i, 16)
            return {"core": gx % 2, "x": (gx // 2) % 8, "y": (gy % 2) * 4 + gx // 16, "z": gy // 2}

        def encode(c):
            return ((c["y"] % 4) * 16 + c["x"] * 2 + c["core"]) * 16 + c["z"] * 2 + c["y"] // 4

        plan = [
            ("x", lambda v: v ^ 1, None),
            ("core", lambda v: v ^ 1, "gx"),
            ("y", lambda v: v ^ 4, "gy"),
            ("x", lambda v: v ^ 2, None),
            ("x", lambda v: 7 - v, None),
            ("y", lambda v: v ^ 1, None),
            ("y", lambda v: v ^ 2, None),
            ("z", lambda v: v ^ 1, None),
            ("z", lambda v: v ^ 2, None),
            ("z", lambda v: 7 - v, None),
        ]
        rounds = []
        for ring, step, tag in plan:
            pairs = []
            for i in range(nx * ny):
                c = decode(i)
                c[ring] = step(c[ring])
                pairs.append((i, encode(c)))
            rounds.append((pairs, tag))
        return rounds
    rounds = []
    for size, stride, tag in ((nx, ny, "gx"), (ny, 1, "gy")):
        for bit in range(size.bit_length() - 1):
            pairs = []
            for i in range(nx * ny):
                index = (i // stride) % size
                pairs.append((i, i + ((index ^ (1 << bit)) - index) * stride))
            rounds.append((pairs, tag if bit == 0 else None))
    return rounds


def from_blocks(blocks, sizex, sizey, sizez):
    lead = blocks.shape[:-2]
    count = len(lead)
    shaped = blocks.reshape(lead + (sizex // 4, sizey // 4, sizez // 4, 4, 4, 4))
    order = list(range(count)) + [count, count + 3, count + 1, count + 4, count + 2, count + 5]
    return shaped.transpose(order).reshape(lead + (sizex, sizey, sizez))


def padded_of(center, xlo, xhi, ylo, yhi):
    sizez = center.shape[-1]
    corner = jnp.zeros(center.shape[:-3] + (1, 1, sizez), center.dtype)
    mid = jnp.concatenate([ylo[..., :, None, :], center, yhi[..., :, None, :]], axis=-2)
    top = jnp.concatenate([corner, xlo[..., None, :, :], corner], axis=-2)
    bot = jnp.concatenate([corner, xhi[..., None, :, :], corner], axis=-2)
    return jnp.concatenate([top, mid, bot], axis=-3)


def padded_laplace(padded, zup, zdown):
    center = padded[1:-1, 1:-1]
    total = padded[2:, 1:-1] + padded[:-2, 1:-1] + padded[1:-1, 2:] + padded[1:-1, :-2]
    total = total + zup + zdown
    return total - 6.0 * center


def z_neighbours(field):
    sizez = field.shape[-1]
    rows = lax.broadcasted_iota(jnp.int32, (sizez, 2 * sizez), 0)
    cols = lax.broadcasted_iota(jnp.int32, (sizez, 2 * sizez), 1)
    source = jnp.where(cols < sizez, (cols + 1) % sizez, (cols - sizez - 1) % sizez)
    shift = (rows == source).astype(field.dtype)
    both = jnp.dot(field.reshape(-1, sizez), shift, precision=lax.Precision.HIGHEST, preferred_element_type=jnp.float32)
    return both[:, :sizez].reshape(field.shape), both[:, sizez:].reshape(field.shape)


def body(velocity, cotangent, block_ids, fluid_count, fluid_cells, w_in, w_mid, w_out):
    sizex, sizey, sizez = velocity.shape
    slots = block_ids.shape[2]
    nblocks = sizex * sizey * sizez // 64
    cells = sizex * sizey * sizez

    xlo = shift_from(velocity[-1], "gx", 1)
    xhi = shift_from(velocity[0], "gx", -1)
    ylo = shift_from(velocity[:, -1], "gy", 1)
    yhi = shift_from(velocity[:, 0], "gy", -1)
    padded = padded_of(velocity, xlo, xhi, ylo, yhi)

    ids = block_ids.reshape(slots)
    live = (jnp.arange(slots) < fluid_count[0, 0]).astype(jnp.bfloat16)
    slot_w = fluid_cells.reshape(slots, 64).astype(jnp.bfloat16) * live[:, None]
    onehot = (ids[:, None] == jnp.arange(nblocks)[None, :]).astype(jnp.bfloat16)
    block_w = lax.dot_general(onehot, slot_w, (((0,), (0,)), ((), ())), preferred_element_type=jnp.float32)
    weight = from_blocks(block_w, sizex, sizey, sizez).reshape(cells)

    center = padded[1:-1, 1:-1]
    vup, vdown = z_neighbours(velocity)
    cup, cdown = z_neighbours(cotangent)
    chosen = jnp.stack(
        [
            center,
            padded[2:, 1:-1],
            padded[:-2, 1:-1],
            padded[1:-1, 2:],
            padded[1:-1, :-2],
            vup,
            vdown,
        ]
    ).astype(jnp.bfloat16).reshape(7, cells)
    h1 = jnp.tanh(jnp.dot(w_in, chosen, preferred_element_type=jnp.float32)).astype(jnp.bfloat16)
    h2 = jnp.tanh(jnp.dot(w_mid, h1, preferred_element_type=jnp.float32)).astype(jnp.bfloat16)
    corr = jnp.dot(w_out, h2, preferred_element_type=jnp.float32)[0] * weight
    dcl = (cotangent.reshape(cells) * weight).astype(jnp.bfloat16)
    h2f = h2.astype(jnp.float32)
    h1f = h1.astype(jnp.float32)
    dh2 = jnp.dot(w_out.T, dcl[None, :], preferred_element_type=jnp.float32)
    da2 = (dh2 * (1.0 - h2f * h2f)).astype(jnp.bfloat16)
    dh1 = jnp.dot(w_mid.T, da2, preferred_element_type=jnp.float32)
    da1 = (dh1 * (1.0 - h1f * h1f)).astype(jnp.bfloat16)
    dfeat = jnp.dot(w_in.T, da1, preferred_element_type=jnp.float32).reshape(7, sizex, sizey, sizez)
    dims = (((1,), (1,)), ((), ()))
    gmid = lax.dot_general(da2, h1, dims, preferred_element_type=jnp.float32)
    gout = lax.dot_general(dcl[None, :], h2, dims, preferred_element_type=jnp.float32)

    new_field = velocity + viscosity * padded_laplace(padded, vup, vdown) + corr.reshape(sizex, sizey, sizez)

    nx = lax.axis_size("gx")
    ny = lax.axis_size("gy")
    xodd = lax.axis_index("gx") % 2 == 1
    yodd = lax.axis_index("gy") % 2 == 1
    up_x, down_x = jnp.stack([dfeat[1, -1], cotangent[-1]]), jnp.stack([dfeat[2, 0], cotangent[0]])
    up_y, down_y = jnp.stack([dfeat[3, :, -1], cotangent[:, -1]]), jnp.stack([dfeat[4, :, 0], cotangent[:, 0]])
    pair_face = {"gx": jnp.where(xodd, down_x, up_x), "gy": jnp.where(yodd, down_y, up_y)}
    other_x = lax.ppermute(
        jnp.where(xodd, up_x, down_x), "gx", [(i, (i + 1) % nx if i % 2 else (i - 1) % nx) for i in range(nx)]
    )
    other_y = lax.ppermute(
        jnp.where(yodd, up_y, down_y), "gy", [(i, (i + 1) % ny if i % 2 else (i - 1) % ny) for i in range(ny)]
    )

    gin_t = lax.dot_general(chosen, da1, dims, preferred_element_type=jnp.float32)
    width = gmid.shape[0]
    lanes = 128
    grads = jnp.concatenate(
        [gmid.reshape(-1, lanes), jnp.concatenate([gin_t, gout], axis=0).reshape(-1, lanes)], axis=0
    )
    received = {}
    for pairs, tag in reduce_rounds(nx, ny):
        if tag is None:
            grads = grads + lax.ppermute(grads, ("gx", "gy"), pairs)
        else:
            rows = grads.shape[0]
            face = pair_face[tag]
            message = jnp.concatenate([grads, face.reshape(-1, grads.shape[1])], axis=0)
            got = lax.ppermute(message, ("gx", "gy"), pairs)
            received[tag] = got[rows:].reshape(face.shape)
            grads = grads + got[:rows]
    from_xlo = jnp.where(xodd, received["gx"], other_x)
    from_xhi = jnp.where(xodd, other_x, received["gx"])
    from_ylo = jnp.where(yodd, received["gy"], other_y)
    from_yhi = jnp.where(yodd, other_y, received["gy"])
    cot_pad = padded_of(cotangent, from_xlo[1], from_xhi[1], from_ylo[1], from_yhi[1])
    from_xlo, from_xhi, from_ylo, from_yhi = from_xlo[0], from_xhi[0], from_ylo[0], from_yhi[0]

    side1 = jnp.concatenate([from_xlo[None], dfeat[1, :-1]], axis=0)
    side2 = jnp.concatenate([dfeat[2, 1:], from_xhi[None]], axis=0)
    side3 = jnp.concatenate([from_ylo[:, None], dfeat[3, :, :-1]], axis=1)
    side4 = jnp.concatenate([dfeat[4, :, 1:], from_yhi[:, None]], axis=1)
    local = dfeat[0] + jnp.roll(dfeat[5], 1, 2) + jnp.roll(dfeat[6], -1, 2)
    grad_field = cotangent + viscosity * padded_laplace(cot_pad, cup, cdown) + local + (side1 + side2 + side3 + side4)

    scale = 1.0 / jnp.sqrt(jnp.float32(nx * ny * slots * 64))
    total = grads * scale
    mid_rows = width * width // lanes
    grad_mid = total[:mid_rows].reshape(width, width)
    rest = total[mid_rows:].reshape(-1, width)
    grad_in = rest[:7].T
    grad_out = rest[7:8]
    return (new_field, grad_field, grad_in, grad_mid, grad_out)


def solution(mesh):
    in_specs = (
        P("gx", "gy", None),
        P("gx", "gy", None),
        P("gx", "gy", None),
        P("gx", "gy"),
        P("gx", "gy", None),
        P(),
        P(),
        P(),
    )
    out_specs = (P("gx", "gy", None), P("gx", "gy", None), P(), P(), P())
    return jax.shard_map(body, mesh=mesh, in_specs=in_specs, out_specs=out_specs, check_vma=False)
```

```python
import jax
import jax.numpy as jnp
from jax import lax
from jax.sharding import PartitionSpec as P

viscosity = 0.1


def shift_from(face, axis, step):
    count = lax.axis_size(axis)
    return lax.ppermute(face, axis, [(i, (i + step) % count) for i in range(count)])


def reduce_rounds(nx, ny):
    if (nx, ny) == (64, 16):
        def decode(i):
            gx, gy = divmod(i, 16)
            return {"core": gx % 2, "x": (gx // 2) % 8, "y": (gy % 2) * 4 + gx // 16, "z": gy // 2}

        def encode(c):
            return ((c["y"] % 4) * 16 + c["x"] * 2 + c["core"]) * 16 + c["z"] * 2 + c["y"] // 4

        plan = [
            ("x", lambda v: v ^ 1, None),
            ("core", lambda v: v ^ 1, "gx"),
            ("y", lambda v: v ^ 4, "gy"),
            ("x", lambda v: v ^ 2, None),
            ("x", lambda v: 7 - v, None),
            ("y", lambda v: v ^ 1, None),
            ("y", lambda v: v ^ 2, None),
            ("z", lambda v: v ^ 1, None),
            ("z", lambda v: v ^ 2, None),
            ("z", lambda v: 7 - v, None),
        ]
        rounds = []
        for ring, step, tag in plan:
            pairs = []
            for i in range(nx * ny):
                c = decode(i)
                c[ring] = step(c[ring])
                pairs.append((i, encode(c)))
            rounds.append((pairs, tag))
        return rounds
    rounds = []
    for size, stride, tag in ((nx, ny, "gx"), (ny, 1, "gy")):
        for bit in range(size.bit_length() - 1):
            pairs = []
            for i in range(nx * ny):
                index = (i // stride) % size
                pairs.append((i, i + ((index ^ (1 << bit)) - index) * stride))
            rounds.append((pairs, tag if bit == 0 else None))
    return rounds


def from_blocks(blocks, sizex, sizey, sizez):
    lead = blocks.shape[:-2]
    count = len(lead)
    shaped = blocks.reshape(lead + (sizex // 4, sizey // 4, sizez // 4, 4, 4, 4))
    order = list(range(count)) + [count, count + 3, count + 1, count + 4, count + 2, count + 5]
    return shaped.transpose(order).reshape(lead + (sizex, sizey, sizez))


def padded_of(center, xlo, xhi, ylo, yhi):
    sizez = center.shape[-1]
    corner = jnp.zeros(center.shape[:-3] + (1, 1, sizez), center.dtype)
    mid = jnp.concatenate([ylo[..., :, None, :], center, yhi[..., :, None, :]], axis=-2)
    top = jnp.concatenate([corner, xlo[..., None, :, :], corner], axis=-2)
    bot = jnp.concatenate([corner, xhi[..., None, :, :], corner], axis=-2)
    return jnp.concatenate([top, mid, bot], axis=-3)


def padded_laplace(padded, zup, zdown):
    center = padded[1:-1, 1:-1]
    total = padded[2:, 1:-1] + padded[:-2, 1:-1] + padded[1:-1, 2:] + padded[1:-1, :-2]
    total = total + zup + zdown
    return total - 6.0 * center


def z_neighbours(field):
    sizez = field.shape[-1]
    rows = lax.broadcasted_iota(jnp.int32, (sizez, 2 * sizez), 0)
    cols = lax.broadcasted_iota(jnp.int32, (sizez, 2 * sizez), 1)
    source = jnp.where(cols < sizez, (cols + 1) % sizez, (cols - sizez - 1) % sizez)
    shift = (rows == source).astype(field.dtype)
    both = jnp.dot(field.reshape(-1, sizez), shift, precision=lax.Precision.HIGHEST, preferred_element_type=jnp.float32)
    return both[:, :sizez].reshape(field.shape), both[:, sizez:].reshape(field.shape)


def body(velocity, cotangent, block_ids, fluid_count, fluid_cells, w_in, w_mid, w_out):
    sizex, sizey, sizez = velocity.shape
    slots = block_ids.shape[2]
    nblocks = sizex * sizey * sizez // 64
    cells = sizex * sizey * sizez

    both = jnp.stack([velocity, cotangent])
    xlo = shift_from(both[:, -1], "gx", 1)
    xhi = shift_from(both[:, 0], "gx", -1)
    ylo = shift_from(both[:, :, -1], "gy", 1)
    yhi = shift_from(both[:, :, 0], "gy", -1)
    padded = padded_of(velocity, xlo[0], xhi[0], ylo[0], yhi[0])
    cot_pad = padded_of(cotangent, xlo[1], xhi[1], ylo[1], yhi[1])

    ids = block_ids.reshape(slots)
    live = (jnp.arange(slots) < fluid_count[0, 0]).astype(jnp.bfloat16)
    slot_w = fluid_cells.reshape(slots, 64).astype(jnp.bfloat16) * live[:, None]
    onehot = (ids[:, None] == jnp.arange(nblocks)[None, :]).astype(jnp.bfloat16)
    block_w = lax.dot_general(onehot, slot_w, (((0,), (0,)), ((), ())), preferred_element_type=jnp.float32)
    weight = from_blocks(block_w, sizex, sizey, sizez).reshape(cells)

    center = padded[1:-1, 1:-1]
    zup, zdown = z_neighbours(both)
    vup, cup = zup[0], zup[1]
    vdown, cdown = zdown[0], zdown[1]
    chosen = jnp.stack(
        [
            center,
            padded[2:, 1:-1],
            padded[:-2, 1:-1],
            padded[1:-1, 2:],
            padded[1:-1, :-2],
            vup,
            vdown,
        ]
    ).astype(jnp.bfloat16).reshape(7, cells)
    h1 = jnp.tanh(jnp.dot(w_in, chosen, preferred_element_type=jnp.float32)).astype(jnp.bfloat16)
    h2 = jnp.tanh(jnp.dot(w_mid, h1, preferred_element_type=jnp.float32)).astype(jnp.bfloat16)
    corr = jnp.dot(w_out, h2, preferred_element_type=jnp.float32)[0] * weight
    dcl = (cotangent.reshape(cells) * weight).astype(jnp.bfloat16)
    h2f = h2.astype(jnp.float32)
    h1f = h1.astype(jnp.float32)
    dh2 = jnp.dot(w_out.T, dcl[None, :], preferred_element_type=jnp.float32)
    da2 = (dh2 * (1.0 - h2f * h2f)).astype(jnp.bfloat16)
    dh1 = jnp.dot(w_mid.T, da2, preferred_element_type=jnp.float32)
    da1 = (dh1 * (1.0 - h1f * h1f)).astype(jnp.bfloat16)
    dfeat = jnp.dot(w_in.T, da1, preferred_element_type=jnp.float32).reshape(7, sizex, sizey, sizez)
    dims = (((1,), (1,)), ((), ()))
    gmid = lax.dot_general(da2, h1, dims, preferred_element_type=jnp.float32)
    gout = lax.dot_general(dcl[None, :], h2, dims, preferred_element_type=jnp.float32)

    new_field = velocity + viscosity * padded_laplace(padded, vup, vdown) + corr.reshape(sizex, sizey, sizez)

    nx = lax.axis_size("gx")
    ny = lax.axis_size("gy")
    xodd = lax.axis_index("gx") % 2 == 1
    yodd = lax.axis_index("gy") % 2 == 1
    up_x, down_x = dfeat[1, -1], dfeat[2, 0]
    up_y, down_y = dfeat[3, :, -1], dfeat[4, :, 0]
    pair_face = {"gx": jnp.where(xodd, down_x, up_x), "gy": jnp.where(yodd, down_y, up_y)}
    other_x = lax.ppermute(
        jnp.where(xodd, up_x, down_x), "gx", [(i, (i + 1) % nx if i % 2 else (i - 1) % nx) for i in range(nx)]
    )
    other_y = lax.ppermute(
        jnp.where(yodd, up_y, down_y), "gy", [(i, (i + 1) % ny if i % 2 else (i - 1) % ny) for i in range(ny)]
    )

    gin_t = lax.dot_general(chosen, da1, dims, preferred_element_type=jnp.float32)
    width = gmid.shape[0]
    lanes = 128
    grads = jnp.concatenate(
        [gmid.reshape(-1, lanes), jnp.concatenate([gin_t, gout], axis=0).reshape(-1, lanes)], axis=0
    )
    received = {}
    for pairs, tag in reduce_rounds(nx, ny):
        if tag is None:
            grads = grads + lax.ppermute(grads, ("gx", "gy"), pairs)
        else:
            rows = grads.shape[0]
            face = pair_face[tag]
            message = jnp.concatenate([grads, face.reshape(-1, grads.shape[1])], axis=0)
            got = lax.ppermute(message, ("gx", "gy"), pairs)
            received[tag] = got[rows:].reshape(face.shape)
            grads = grads + got[:rows]
    from_xlo = jnp.where(xodd, received["gx"], other_x)
    from_xhi = jnp.where(xodd, other_x, received["gx"])
    from_ylo = jnp.where(yodd, received["gy"], other_y)
    from_yhi = jnp.where(yodd, other_y, received["gy"])

    side1 = jnp.concatenate([from_xlo[None], dfeat[1, :-1]], axis=0)
    side2 = jnp.concatenate([dfeat[2, 1:], from_xhi[None]], axis=0)
    side3 = jnp.concatenate([from_ylo[:, None], dfeat[3, :, :-1]], axis=1)
    side4 = jnp.concatenate([dfeat[4, :, 1:], from_yhi[:, None]], axis=1)
    local = dfeat[0] + jnp.roll(dfeat[5], 1, 2) + jnp.roll(dfeat[6], -1, 2)
    grad_field = cotangent + viscosity * padded_laplace(cot_pad, cup, cdown) + local + (side1 + side2 + side3 + side4)

    scale = 1.0 / jnp.sqrt(jnp.float32(nx * ny * slots * 64))
    total = grads * scale
    mid_rows = width * width // lanes
    grad_mid = total[:mid_rows].reshape(width, width)
    rest = total[mid_rows:].reshape(-1, width)
    grad_in = rest[:7].T
    grad_out = rest[7:8]
    return (new_field, grad_field, grad_in, grad_mid, grad_out)


def solution(mesh):
    in_specs = (
        P("gx", "gy", None),
        P("gx", "gy", None),
        P("gx", "gy", None),
        P("gx", "gy"),
        P("gx", "gy", None),
        P(),
        P(),
        P(),
    )
    out_specs = (P("gx", "gy", None), P("gx", "gy", None), P(), P(), P())
    return jax.shard_map(body, mesh=mesh, in_specs=in_specs, out_specs=out_specs, check_vma=False)
```
